128 devices in a mesh: gx: 128 (over y, x, z, core).
Axes of the slice: x: 4, y: 4, z: 4, core: 2. Of those that a mesh axis runs over, the one named last changes fastest.
Arguments:
- right_side: float32 [1024, 256, 256], P('gx'), may hold values from -6 to 6, as said below
- density: float32 [1024, 256, 256], P('gx'), may hold values from 0.25 to 4
Outputs:
- pressure: float32 [1024, 256, 256], P('gx')
- pending: float32 [1024, 256, 256], P('gx')
The draws below stay inside these ranges and needn't reach their ends.
Inputs may be any that keep to these rules, and one draw needn't show every extreme that they name: `right_side`: rough values in every cell.
All inputs are finite; a program needn't handle non-finite values.
Results may differ from the reference program's by a relative error of at most 0.0003.
Values sent between devices are 32-bit elements; how exact they have to be, the bound alone decides.
No kernel may reach another device: no remote copies, remote signals or barrier semaphores. Data moves between devices by JAX's collectives and lax.ppermute only.
A program may use at most 128 MiB of HBM per device.

```python
import math
import jax
import jax.numpy as jnp

SIDE = 256
SWEEPS = 3
TOP_SWEEPS = 6
CYCLES = 2
NX = 1024


def draw_right_side(key, part):
    shape = (NX, SIDE, SIDE)
    return jnp.clip(jax.random.normal(key, shape, jnp.float32), -6.0, 6.0)


def level_of(rng, extent, shards, least, high):
    loudness = 1.0
    for axis_at, blocks in shards:
        draws = jax.random.uniform(jax.random.fold_in(jax.random.fold_in(rng, 6), axis_at), (blocks,), jnp.float32, least / len(shards), high / len(shards))
        loudness = loudness * jnp.repeat(jnp.exp(draws), extent[axis_at] // blocks).reshape((-1,) + (1,) * (len(extent) - 1 - axis_at))
    return loudness


def setup_inputs(seed: int = 0) -> dict:
    arg_keys = jax.random.split(jax.random.key(seed), 3)
    right_side = draw_right_side(jax.random.fold_in(arg_keys[2], 71), 0)
    density = jnp.clip(jnp.exp(math.log(4.0) - 2.7725887 * jax.random.uniform(arg_keys[1], (NX, SIDE, SIDE), jnp.float32) ** level_of(arg_keys[1], (NX, SIDE, SIDE), ((0, 128),), -0.2, 0.2)), 0.25, 4.0)
    return {"right_side": right_side, "density": density}


OMEGA = 0.8


def coarsen(field):
    extent_x, extent_y, extent_z = field.shape
    shaped = field.reshape(extent_x // 2, 2, extent_y // 2, 2, extent_z // 2, 2)
    return shaped.sum(axis=(1, 3, 5)) * 0.125


def refine(field):
    extent_x, extent_y, extent_z = field.shape
    spread = jnp.broadcast_to(field[:, None, :, None, :, None], (extent_x, 2, extent_y, 2, extent_z, 2))
    return spread.reshape(2 * extent_x, 2 * extent_y, 2 * extent_z)


def neighbours(padded):
    return [padded[:-2, 1:-1, 1:-1], padded[2:, 1:-1, 1:-1], padded[1:-1, :-2, 1:-1],
            padded[1:-1, 2:, 1:-1], padded[1:-1, 1:-1, :-2], padded[1:-1, 1:-1, 2:]]


def make_coefs(rho_planes, inv_spacing):
    center = rho_planes[1:-1]
    safe_rho = jnp.where(center > 0, center, 1.0)
    padded = jnp.pad(rho_planes, ((0, 0), (1, 1), (1, 1)), mode="edge")
    coefs = [(2.0 * inv_spacing) / (safe_rho + jnp.where(nearby > 0, nearby, safe_rho)) for nearby in neighbours(padded)]
    diagonal = coefs[0] + coefs[1] + coefs[2] + coefs[3] + coefs[4] + coefs[5]
    return coefs, diagonal


def apply_op(field_planes, coefs):
    padded = jnp.pad(field_planes, ((0, 0), (1, 1), (1, 1)))
    center = padded[1:-1, 1:-1, 1:-1]
    nearby = neighbours(padded)
    applied = coefs[0] * (center - nearby[0])
    for face in range(1, 6):
        applied = applied + coefs[face] * (center - nearby[face])
    return applied


def pad_planes(field):
    return jnp.pad(field, ((1, 1), (0, 0), (0, 0)))


def smooth(resid, coefs, diagonal, sweeps, extend):
    update = OMEGA * resid / diagonal
    for sweep_no in range(sweeps - 1):
        update = update + OMEGA * (resid - apply_op(extend(update), coefs)) / diagonal
    return update


def reference(right_side, density):
    densities = [density]
    for level_no in range(1, 5):
        densities.append(coarsen(densities[-1]))
    levels = [make_coefs(pad_planes(densities[level_no]), 0.25 ** level_no) for level_no in range(5)]
    pressure = jnp.zeros_like(right_side)
    pending = jnp.zeros_like(right_side)
    for cycle_num in range(CYCLES):
        resid = right_side - apply_op(pad_planes(pressure), levels[0][0])
        residuals = [resid]
        for level_no in range(1, 5):
            residuals.append(coarsen(residuals[-1]))
        fine_part = smooth(residuals[0], levels[0][0], levels[0][1], SWEEPS, pad_planes)
        summed = smooth(residuals[4], levels[4][0], levels[4][1], TOP_SWEEPS, pad_planes)
        for level_no in (3, 2, 1):
            summed = refine(summed) + smooth(residuals[level_no], levels[level_no][0], levels[level_no][1], SWEEPS, pad_planes)
        coarse = refine(summed)
        pressure = pressure + fine_part + pending
        pending = coarse
    return pressure, pending
```

```python
import math

import jax
import jax.numpy as jnp
from jax import lax
from jax.sharding import PartitionSpec as P

SWEEPS = 3
TOP_SWEEPS = 6
CYCLES = 2


OMEGA = 0.8
EXACT = lax.Precision.HIGHEST


def recv(value, steps, cyclic):
    count = lax.axis_size("gx")
    if cyclic:
        pairs = [(i, (i + steps) % count) for i in range(count)]
    else:
        pairs = [(i, i + steps) for i in range(count) if 0 <= i + steps < count]
    return lax.ppermute(value, "gx", pairs)


def inside(per_device, ghosts, length):
    count = lax.axis_size("gx")
    first = lax.axis_index("gx") * per_device - ghosts
    index = first + jnp.arange(length, dtype=jnp.int32)
    keep = (index >= 0) & (index < count * per_device)
    return keep.astype(jnp.float32)[:, None, None]


def exchange(to_right, to_left, steps, cyclic=False):
    arrays_r, arrays_l = list(to_right), list(to_left)
    shapes = [a.shape for a in arrays_r]
    stacked = all(shape[1:] == shapes[0][1:] for shape in shapes)
    if stacked:
        flat_r = jnp.concatenate(arrays_r)
        flat_l = jnp.concatenate(arrays_l)
    else:
        flat_r = jnp.concatenate([a.reshape(-1) for a in arrays_r])
        flat_l = jnp.concatenate([a.reshape(-1) for a in arrays_l])
    got_l, got_r = recv(flat_r, steps, cyclic), recv(flat_l, -steps, cyclic)

    def split(flat):
        out, at = [], 0
        for shape in shapes:
            if stacked:
                out.append(flat[at:at + shape[0]])
                at += shape[0]
            else:
                size = math.prod(shape)
                out.append(flat[at:at + size].reshape(shape))
                at += size
        return out

    return split(got_l), split(got_r)


def pair_matrix(extent):
    rows = jnp.arange(extent, dtype=jnp.int32)[:, None] // 2
    cols = jnp.arange(extent // 2, dtype=jnp.int32)[None, :]
    return (rows == cols).astype(jnp.float32)


def shrink_sides(field):
    extent_y = field.shape[1]
    extent_z = field.shape[2]
    along_z = jnp.einsum("xyz,zw->xyw", field, pair_matrix(extent_z), precision=EXACT)
    return jnp.einsum("xyw,yv->xvw", along_z, pair_matrix(extent_y), precision=EXACT)


def grow_sides(field):
    extent_y = field.shape[1]
    extent_z = field.shape[2]
    along_z = jnp.einsum("xyw,zw->xyz", field, pair_matrix(2 * extent_z), precision=EXACT)
    return jnp.einsum("xvz,yv->xyz", along_z, pair_matrix(2 * extent_y), precision=EXACT)


def coarsen(field):
    extent_x, extent_y, extent_z = field.shape
    planes = field.reshape(extent_x // 2, 2, extent_y, extent_z).sum(axis=1)
    return shrink_sides(planes) * 0.125


def refine(field):
    extent_x, extent_y, extent_z = field.shape
    wider = grow_sides(field)
    spread = jnp.broadcast_to(wider[:, None], (extent_x, 2, 2 * extent_y, 2 * extent_z))
    return spread.reshape(2 * extent_x, 2 * extent_y, 2 * extent_z)


def make_coefs(rho_ext, inv_spacing):
    two_s = 2.0 * inv_spacing
    center = rho_ext[1:-1]
    safe = jnp.where(center > 0, center, 1.0)
    padded = jnp.pad(center, ((0, 0), (1, 1), (1, 1)), mode="edge")
    near = [
        rho_ext[:-2],
        rho_ext[2:],
        padded[:, :-2, 1:-1],
        padded[:, 2:, 1:-1],
        padded[:, 1:-1, :-2],
        padded[:, 1:-1, 2:],
    ]
    faces = [two_s / (safe + jnp.where(nb > 0, nb, safe)) for nb in near]
    diag = faces[0] + faces[1] + faces[2] + faces[3] + faces[4] + faces[5]
    lo, hi = rho_ext[:-1], rho_ext[1:]
    kxo = jnp.where((lo > 0) & (hi > 0), two_s / (lo + hi), 0.0)
    return {
        "kxo": kxo,
        "kyl": faces[2],
        "kyh": faces[3],
        "kzl": faces[4],
        "kzh": faces[5],
        "w": OMEGA / diag,
        "diag": diag,
    }


def side_terms(field, co, lo, hi):
    padded = jnp.pad(field, ((0, 0), (1, 1), (1, 1)))
    return (
        co["kyl"][lo:hi] * padded[:, :-2, 1:-1]
        + co["kyh"][lo:hi] * padded[:, 2:, 1:-1]
        + co["kzl"][lo:hi] * padded[:, 1:-1, :-2]
        + co["kzh"][lo:hi] * padded[:, 1:-1, 2:]
    )


def smooth(resid, co, sweeps):
    length = resid.shape[0]
    kxo = co["kxo"][1:-1]
    update = co["w"] * resid
    for sweep_no in range(1, sweeps):
        lo, hi = sweep_no, length - sweep_no
        inner = update[1:-1]
        off = (
            kxo[lo - 1:hi - 1] * update[:-2]
            + kxo[lo:hi] * update[2:]
            + side_terms(inner, co, lo, hi)
        )
        update = (1.0 - OMEGA) * inner + co["w"][lo:hi] * (resid[lo:hi] + off)
    return update


def per_device(right_side, density):
    me = lax.axis_index("gx")

    (dl, rl), (dr, rr) = exchange(
        [density[-3:], right_side[-2:]], [density[:3], right_side[:2]], 1
    )
    rho0_ext = jnp.concatenate([dl, density, dr])
    rhs_ext = jnp.concatenate([rl, right_side, rr])
    co0 = make_coefs(rho0_ext, 1.0)

    rho1 = coarsen(density)
    rho2 = coarsen(rho1)
    rho3 = coarsen(rho2)

    def restrict(resid):
        r1 = coarsen(resid)
        r2 = coarsen(r1)
        return r1, r2, coarsen(r2)

    def gather_coarse(r1, r2, r3, with_rho):
        to_right = [r1[-2:], r2, r3]
        to_left = [r1[:2], r2, r3]
        if with_rho:
            to_right += [rho1[-3:], rho2, rho3]
            to_left += [rho1[:3], rho2, rho3]
        got_l, got_r = exchange(to_right, to_left, 1, True)
        r1e = jnp.concatenate([got_l[0], r1, got_r[0]])
        r2e = jnp.concatenate([got_l[1], r2, got_r[1]])
        win3 = [jnp.concatenate([got_l[2], r3, got_r[2]])]
        extra = {}
        if with_rho:
            extra["rho1e"] = jnp.concatenate([got_l[3], rho1, got_r[3]])
            rho2_l, rho2_r = got_l[4], got_r[4]
            win3.append(jnp.concatenate([got_l[5], rho3, got_r[5]]))
        to_right = list(win3)
        to_left = list(win3)
        if with_rho:
            to_right.append(rho2_r[-1:])
            to_left.append(rho2_l[:1])
        got_l, got_r = exchange(to_right, to_left, 3, True)
        win9 = [jnp.concatenate([got_l[k], win3[k], got_r[k]]) for k in range(len(win3))]
        if with_rho:
            extra["rho2e"] = jnp.concatenate([got_l[-1], rho2_l, rho2, rho2_r, got_r[-1]])
        got_l, got_r = exchange(win9, win9, 9, True)
        win27 = [jnp.concatenate([got_l[k], win9[k], got_r[k]]) for k in range(len(win9))]
        win27 = [part * inside(1, 13, 27) for part in win27]
        r1e = r1e * inside(4, 2, r1e.shape[0])
        r2e = r2e * inside(2, 2, r2e.shape[0])
        if with_rho:
            extra["rho1e"] = extra["rho1e"] * inside(4, 3, extra["rho1e"].shape[0])
            extra["rho2e"] = extra["rho2e"] * inside(2, 3, extra["rho2e"].shape[0])
        return r1e, r2e, win27, extra

    r1, r2, r3 = restrict(right_side)
    r1e, r2e, win, extra = gather_coarse(r1, r2, r3, True)
    r3w, rho3w = win
    co1 = make_coefs(extra["rho1e"], 0.25)
    co2 = make_coefs(extra["rho2e"], 0.25**2)
    center = 13
    co3 = make_coefs(rho3w[center - 3:center + 4], 0.25**3)
    pair_start = 1 - me % 2

    def to_top(window):
        return coarsen(lax.dynamic_slice_in_dim(window, pair_start, 2 * center))

    co4 = make_coefs(to_top(rho3w), 0.25**4)

    def coarse_part(r1e, r2e, r3w):
        top = smooth(to_top(r3w)[1:-1], co4, TOP_SWEEPS)
        summed = grow_sides(top) + smooth(r3w[center - 2:center + 3], co3, SWEEPS)
        summed = refine(summed) + smooth(r2e, co2, SWEEPS)
        summed = refine(summed) + smooth(r1e, co1, SWEEPS)
        return refine(summed)

    fine_0 = smooth(rhs_ext, co0, SWEEPS)
    coarse_0 = coarse_part(r1e, r2e, r3w)

    (fl,), (fr,) = exchange([fine_0[-3:]], [fine_0[:3]], 1)
    fine_ext = jnp.concatenate([fl, fine_0, fr])
    applied_off = (
        co0["kxo"][:-1] * fine_ext[:-2]
        + co0["kxo"][1:] * fine_ext[2:]
        + side_terms(fine_ext[1:-1], co0, 0, fine_ext.shape[0] - 2)
    )
    resid_ext = rhs_ext - (co0["diag"] * fine_ext[1:-1] - applied_off)
    fine_1 = smooth(resid_ext, co0, SWEEPS)
    r1, r2, r3 = restrict(resid_ext[2:-2])
    r1e, r2e, win, _ = gather_coarse(r1, r2, r3, False)
    coarse_1 = coarse_part(r1e, r2e, win[0])

    pressure = (fine_0 + fine_1) + coarse_0
    return (pressure, coarse_1)


def solution(mesh):
    return jax.shard_map(
        per_device,
        mesh=mesh,
        in_specs=(P("gx", None, None), P("gx", None, None)),
        out_specs=(P("gx", None, None), P("gx", None, None)),
        check_vma=False,
    )
```

```python
import math

import jax
import jax.numpy as jnp
from jax import lax
from jax.experimental import pallas as pl
from jax.experimental.pallas import tpu as pltpu
from jax.sharding import PartitionSpec as P

SWEEPS = 3
TOP_SWEEPS = 6
CYCLES = 2


OMEGA = 0.8
EXACT = lax.Precision.HIGHEST


def recv(value, steps, cyclic):
    count = lax.axis_size("gx")
    if cyclic:
        pairs = [(i, (i + steps) % count) for i in range(count)]
    else:
        pairs = [(i, i + steps) for i in range(count) if 0 <= i + steps < count]
    return lax.ppermute(value, "gx", pairs)


def inside(per_device, ghosts, length):
    count = lax.axis_size("gx")
    first = lax.axis_index("gx") * per_device - ghosts
    index = first + jnp.arange(length, dtype=jnp.int32)
    keep = (index >= 0) & (index < count * per_device)
    return keep.astype(jnp.float32)[:, None, None]


def exchange(to_right, to_left, steps, cyclic=False):
    arrays_r, arrays_l = list(to_right), list(to_left)
    shapes = [a.shape for a in arrays_r]
    stacked = all(shape[1:] == shapes[0][1:] for shape in shapes)
    if stacked:
        flat_r = jnp.concatenate(arrays_r)
        flat_l = jnp.concatenate(arrays_l)
    else:
        flat_r = jnp.concatenate([a.reshape(-1) for a in arrays_r])
        flat_l = jnp.concatenate([a.reshape(-1) for a in arrays_l])
    got_l, got_r = recv(flat_r, steps, cyclic), recv(flat_l, -steps, cyclic)

    def split(flat):
        out, at = [], 0
        for shape in shapes:
            if stacked:
                out.append(flat[at:at + shape[0]])
                at += shape[0]
            else:
                size = math.prod(shape)
                out.append(flat[at:at + size].reshape(shape))
                at += size
        return out

    return split(got_l), split(got_r)


def pair_matrix(extent):
    rows = jnp.arange(extent, dtype=jnp.int32)[:, None] // 2
    cols = jnp.arange(extent // 2, dtype=jnp.int32)[None, :]
    return (rows == cols).astype(jnp.float32)


def shrink_sides(field):
    extent_y = field.shape[1]
    extent_z = field.shape[2]
    along_z = jnp.einsum("xyz,zw->xyw", field, pair_matrix(extent_z), precision=EXACT)
    return jnp.einsum("xyw,yv->xvw", along_z, pair_matrix(extent_y), precision=EXACT)


def grow_sides(field):
    extent_y = field.shape[1]
    extent_z = field.shape[2]
    along_z = jnp.einsum("xyw,zw->xyz", field, pair_matrix(2 * extent_z), precision=EXACT)
    return jnp.einsum("xvz,yv->xyz", along_z, pair_matrix(2 * extent_y), precision=EXACT)


def coarsen(field):
    extent_x, extent_y, extent_z = field.shape
    planes = field.reshape(extent_x // 2, 2, extent_y, extent_z).sum(axis=1)
    return shrink_sides(planes) * 0.125


def refine(field):
    extent_x, extent_y, extent_z = field.shape
    wider = grow_sides(field)
    spread = jnp.broadcast_to(wider[:, None], (extent_x, 2, 2 * extent_y, 2 * extent_z))
    return spread.reshape(2 * extent_x, 2 * extent_y, 2 * extent_z)


def make_coefs(rho_ext, inv_spacing):
    two_s = 2.0 * inv_spacing
    center = rho_ext[1:-1]
    safe = jnp.where(center > 0, center, 1.0)
    padded = jnp.pad(center, ((0, 0), (1, 1), (1, 1)), mode="edge")
    near = [
        rho_ext[:-2],
        rho_ext[2:],
        padded[:, :-2, 1:-1],
        padded[:, 2:, 1:-1],
        padded[:, 1:-1, :-2],
        padded[:, 1:-1, 2:],
    ]
    faces = [two_s / (safe + jnp.where(nb > 0, nb, safe)) for nb in near]
    diag = faces[0] + faces[1] + faces[2] + faces[3] + faces[4] + faces[5]
    lo, hi = rho_ext[:-1], rho_ext[1:]
    kxo = jnp.where((lo > 0) & (hi > 0), two_s / (lo + hi), 0.0)
    return {
        "kxo": kxo,
        "kyl": faces[2],
        "kyh": faces[3],
        "kzl": faces[4],
        "kzh": faces[5],
        "w": OMEGA / diag,
        "diag": diag,
    }


def side_terms(field, co, lo, hi):
    padded = jnp.pad(field, ((0, 0), (1, 1), (1, 1)))
    return (
        co["kyl"][lo:hi] * padded[:, :-2, 1:-1]
        + co["kyh"][lo:hi] * padded[:, 2:, 1:-1]
        + co["kzl"][lo:hi] * padded[:, 1:-1, :-2]
        + co["kzh"][lo:hi] * padded[:, 1:-1, 2:]
    )


def smooth(resid, co, sweeps):
    length = resid.shape[0]
    kxo = co["kxo"][1:-1]
    update = co["w"] * resid
    for sweep_no in range(1, sweeps):
        lo, hi = sweep_no, length - sweep_no
        inner = update[1:-1]
        off = (
            kxo[lo - 1:hi - 1] * update[:-2]
            + kxo[lo:hi] * update[2:]
            + side_terms(inner, co, lo, hi)
        )
        update = (1.0 - OMEGA) * inner + co["w"][lo:hi] * (resid[lo:hi] + off)
    return update


ROWS = 16
PAD = 8
VMEM_LIMIT = 64 * 1024 * 1024


def _zero_pads(buf):
    extent_y, extent_z = buf.shape[1] - 2 * PAD, buf.shape[2]
    zeros = jnp.zeros((PAD, extent_z), jnp.float32)

    def body(p, carry):
        buf[p, pl.ds(0, PAD), :] = zeros
        buf[p, pl.ds(PAD + extent_y, PAD), :] = zeros
        return carry

    lax.fori_loop(0, buf.shape[0], body, 0)


def _plane_loop(first, last, extent_y, body):
    chunks = extent_y // ROWS

    def step(i, carry):
        q = first + i // chunks
        y0 = pl.multiple_of((i % chunks) * ROWS, ROWS)
        body(q, y0)
        return carry

    lax.fori_loop(0, (last - first) * chunks, step, 0)


def _neighbour_sum(src, at, y0, kxo_lo, kxo_hi, kyl, kyh, kzl, kzh):
    extent_z = src.shape[2]
    center = src[at, pl.ds(PAD + y0, ROWS), :]
    below = pltpu.roll(src[at, pl.ds(y0, ROWS + PAD), :], 1, 0)[PAD:PAD + ROWS]
    above = pltpu.roll(src[at, pl.ds(PAD + y0, ROWS + PAD), :], ROWS + PAD - 1, 0)[:ROWS]
    left = pltpu.roll(center, 1, 1)
    right = pltpu.roll(center, extent_z - 1, 1)
    off = (
        kxo_lo * src[at - 1, pl.ds(PAD + y0, ROWS), :]
        + kxo_hi * src[at + 1, pl.ds(PAD + y0, ROWS), :]
        + kyl * below
        + kyh * above
        + kzl * left
        + kzh * right
    )
    return center, off


def _smooth_in_vmem(resid, kxo, kyl, kyh, kzl, kzh, w, out, bufs, sweeps):
    length, extent_y = resid.shape[0], resid.shape[1]
    for buf in bufs:
        _zero_pads(buf)

    def first(q, y0):
        rows = pl.ds(y0, ROWS)
        bufs[0][q, pl.ds(PAD + y0, ROWS), :] = w[q, rows, :] * resid[q, rows, :]

    _plane_loop(0, length, extent_y, first)
    for sweep_no in range(1, sweeps):
        src = bufs[(sweep_no - 1) % 2]
        src_at = sweep_no - 1
        last = sweep_no == sweeps - 1
        dst = out if last else bufs[sweep_no % 2]
        dst_at = sweep_no

        def body(q, y0, src=src, src_at=src_at, dst=dst, dst_at=dst_at, last=last):
            rows = pl.ds(y0, ROWS)
            center, off = _neighbour_sum(
                src, q - src_at, y0, kxo[q - 1, rows, :], kxo[q, rows, :],
                kyl[q, rows, :], kyh[q, rows, :], kzl[q, rows, :], kzh[q, rows, :],
            )
            new = (1.0 - OMEGA) * center + w[q, rows, :] * (resid[q, rows, :] + off)
            if last:
                dst[q - dst_at, rows, :] = new
            else:
                dst[q - dst_at, pl.ds(PAD + y0, ROWS), :] = new

        _plane_loop(sweep_no, length - sweep_no, extent_y, body)


def _fine_first_kernel(resid, kxo, kyl, kyh, kzl, kzh, w, out, buf_a, buf_b):
    _smooth_in_vmem(resid, kxo, kyl, kyh, kzl, kzh, w, out, (buf_a, buf_b), SWEEPS)


def _fine_second_kernel(
    fine_ext, rhs, kxo_full, kyl, kyh, kzl, kzh, w, diag, out, resid_out, held, resid, buf_a, buf_b
):
    planes, extent_y = fine_ext.shape[0], fine_ext.shape[1]
    _zero_pads(held)

    def copy_in(q, y0):
        held[q, pl.ds(PAD + y0, ROWS), :] = fine_ext[q, pl.ds(y0, ROWS), :]

    _plane_loop(0, planes, extent_y, copy_in)

    def residual(q, y0):
        rows = pl.ds(y0, ROWS)
        center, off = _neighbour_sum(
            held, q + 1, y0, kxo_full[q, rows, :], kxo_full[q + 1, rows, :],
            kyl[q, rows, :], kyh[q, rows, :], kzl[q, rows, :], kzh[q, rows, :],
        )
        resid[q, rows, :] = rhs[q, rows, :] - (diag[q, rows, :] * center - off)

    _plane_loop(0, planes - 2, extent_y, residual)
    ghosts = SWEEPS - 1

    def copy_out(q, y0):
        rows = pl.ds(y0, ROWS)
        resid_out[q - ghosts, rows, :] = resid[q, rows, :]

    _plane_loop(ghosts, planes - 2 - ghosts, extent_y, copy_out)
    _smooth_in_vmem(
        resid, kxo_full.at[1:-1], kyl, kyh, kzl, kzh, w, out, (buf_a, buf_b), SWEEPS
    )


def _vmem_call(kernel, outs, scratch, *args):
    return pl.pallas_call(
        kernel,
        out_shape=outs,
        in_specs=[pl.BlockSpec(memory_space=pltpu.VMEM)] * len(args),
        out_specs=(
            [pl.BlockSpec(memory_space=pltpu.VMEM)] * len(outs)
            if isinstance(outs, (list, tuple))
            else pl.BlockSpec(memory_space=pltpu.VMEM)
        ),
        scratch_shapes=scratch,
        compiler_params=pltpu.CompilerParams(vmem_limit_bytes=VMEM_LIMIT),
    )(*args)


def fine_coefs(co):
    extent_y, extent_z = co["kyl"].shape[1], co["kyl"].shape[2]
    ys = jnp.arange(extent_y, dtype=jnp.int32)[None, :, None]
    zs = jnp.arange(extent_z, dtype=jnp.int32)[None, None, :]
    return {
        "kyl": jnp.where(ys == 0, 0.0, co["kyl"]),
        "kyh": jnp.where(ys == extent_y - 1, 0.0, co["kyh"]),
        "kzl": jnp.where(zs == 0, 0.0, co["kzl"]),
        "kzh": jnp.where(zs == extent_z - 1, 0.0, co["kzh"]),
    }


def fine_smooth(resid_ext, co, fc):
    length, extent_y, extent_z = resid_ext.shape
    out = jax.ShapeDtypeStruct((length - 2 * (SWEEPS - 1), extent_y, extent_z), jnp.float32)
    padded = lambda planes: pltpu.VMEM((planes, extent_y + 2 * PAD, extent_z), jnp.float32)
    return _vmem_call(
        _fine_first_kernel, out, [padded(length), padded(length - 2)],
        resid_ext, co["kxo"][1:-1], fc["kyl"], fc["kyh"], fc["kzl"], fc["kzh"], co["w"],
    )


def fine_second(fine_ext, rhs_ext, co, fc):
    planes, extent_y, extent_z = fine_ext.shape
    length = planes - 2
    block = length - 2 * (SWEEPS - 1)
    outs = [jax.ShapeDtypeStruct((block, extent_y, extent_z), jnp.float32)] * 2
    padded = lambda n: pltpu.VMEM((n, extent_y + 2 * PAD, extent_z), jnp.float32)
    return _vmem_call(
        _fine_second_kernel, outs,
        [padded(planes), pltpu.VMEM((length, extent_y, extent_z), jnp.float32),
         padded(length), padded(length - 2)],
        fine_ext, rhs_ext, co["kxo"], fc["kyl"], fc["kyh"], fc["kzl"], fc["kzh"], co["w"], co["diag"],
    )


def per_device(right_side, density):
    me = lax.axis_index("gx")

    (dl, rl), (dr, rr) = exchange(
        [density[-3:], right_side[-2:]], [density[:3], right_side[:2]], 1
    )
    rho0_ext = jnp.concatenate([dl, density, dr])
    rhs_ext = jnp.concatenate([rl, right_side, rr])
    co0 = make_coefs(rho0_ext, 1.0)

    rho1 = coarsen(density)
    rho2 = coarsen(rho1)
    rho3 = coarsen(rho2)

    def restrict(resid):
        r1 = coarsen(resid)
        r2 = coarsen(r1)
        return r1, r2, coarsen(r2)

    def gather_coarse(r1, r2, r3, with_rho):
        to_right = [r1[-2:], r2, r3]
        to_left = [r1[:2], r2, r3]
        if with_rho:
            to_right += [rho1[-3:], rho2, rho3]
            to_left += [rho1[:3], rho2, rho3]
        got_l, got_r = exchange(to_right, to_left, 1, True)
        r1e = jnp.concatenate([got_l[0], r1, got_r[0]])
        r2e = jnp.concatenate([got_l[1], r2, got_r[1]])
        win3 = [jnp.concatenate([got_l[2], r3, got_r[2]])]
        extra = {}
        if with_rho:
            extra["rho1e"] = jnp.concatenate([got_l[3], rho1, got_r[3]])
            rho2_l, rho2_r = got_l[4], got_r[4]
            win3.append(jnp.concatenate([got_l[5], rho3, got_r[5]]))
        to_right = list(win3)
        to_left = list(win3)
        if with_rho:
            to_right.append(rho2_r[-1:])
            to_left.append(rho2_l[:1])
        got_l, got_r = exchange(to_right, to_left, 3, True)
        win9 = [jnp.concatenate([got_l[k], win3[k], got_r[k]]) for k in range(len(win3))]
        if with_rho:
            extra["rho2e"] = jnp.concatenate([got_l[-1], rho2_l, rho2, rho2_r, got_r[-1]])
        got_l, got_r = exchange(win9, win9, 9, True)
        win27 = [jnp.concatenate([got_l[k], win9[k], got_r[k]]) for k in range(len(win9))]
        win27 = [part * inside(1, 13, 27) for part in win27]
        r1e = r1e * inside(4, 2, r1e.shape[0])
        r2e = r2e * inside(2, 2, r2e.shape[0])
        if with_rho:
            extra["rho1e"] = extra["rho1e"] * inside(4, 3, extra["rho1e"].shape[0])
            extra["rho2e"] = extra["rho2e"] * inside(2, 3, extra["rho2e"].shape[0])
        return r1e, r2e, win27, extra

    r1, r2, r3 = restrict(right_side)
    r1e, r2e, win, extra = gather_coarse(r1, r2, r3, True)
    r3w, rho3w = win
    co1 = make_coefs(extra["rho1e"], 0.25)
    co2 = make_coefs(extra["rho2e"], 0.25**2)
    center = 13
    co3 = make_coefs(rho3w[center - 3:center + 4], 0.25**3)
    pair_start = 1 - me % 2

    def to_top(window):
        return coarsen(lax.dynamic_slice_in_dim(window, pair_start, 2 * center))

    co4 = make_coefs(to_top(rho3w), 0.25**4)

    def coarse_part(r1e, r2e, r3w):
        top = smooth(to_top(r3w)[1:-1], co4, TOP_SWEEPS)
        summed = grow_sides(top) + smooth(r3w[center - 2:center + 3], co3, SWEEPS)
        summed = refine(summed) + smooth(r2e, co2, SWEEPS)
        summed = refine(summed) + smooth(r1e, co1, SWEEPS)
        return refine(summed)

    fc0 = fine_coefs(co0)
    fine_0 = fine_smooth(rhs_ext, co0, fc0)
    coarse_0 = coarse_part(r1e, r2e, r3w)

    (fl,), (fr,) = exchange([fine_0[-3:]], [fine_0[:3]], 1)
    fine_ext = jnp.concatenate([fl, fine_0, fr])
    fine_1, resid_block = fine_second(fine_ext, rhs_ext, co0, fc0)
    r1, r2, r3 = restrict(resid_block)
    r1e, r2e, win, _ = gather_coarse(r1, r2, r3, False)
    coarse_1 = coarse_part(r1e, r2e, win[0])

    pressure = (fine_0 + fine_1) + coarse_0
    return (pressure, coarse_1)


def solution(mesh):
    return jax.shard_map(
        per_device,
        mesh=mesh,
        in_specs=(P("gx", None, None), P("gx", None, None)),
        out_specs=(P("gx", None, None), P("gx", None, None)),
        check_vma=False,
    )
```

```python
import math

import jax
import jax.numpy as jnp
from jax import lax
from jax.experimental import pallas as pl
from jax.experimental.pallas import tpu as pltpu
from jax.sharding import PartitionSpec as P

SWEEPS = 3
TOP_SWEEPS = 6
CYCLES = 2


OMEGA = 0.8
EXACT = lax.Precision.HIGHEST


def recv(value, steps, cyclic):
    count = lax.axis_size("gx")
    if cyclic:
        pairs = [(i, (i + steps) % count) for i in range(count)]
    else:
        pairs = [(i, i + steps) for i in range(count) if 0 <= i + steps < count]
    return lax.ppermute(value, "gx", pairs)


def inside(per_device, ghosts, length):
    count = lax.axis_size("gx")
    first = lax.axis_index("gx") * per_device - ghosts
    index = first + jnp.arange(length, dtype=jnp.int32)
    keep = (index >= 0) & (index < count * per_device)
    return keep.astype(jnp.float32)[:, None, None]


def exchange(to_right, to_left, steps, cyclic=False):
    arrays_r, arrays_l = list(to_right), list(to_left)
    shapes = [a.shape for a in arrays_r]
    stacked = all(shape[1:] == shapes[0][1:] for shape in shapes)
    if stacked:
        flat_r = jnp.concatenate(arrays_r)
        flat_l = jnp.concatenate(arrays_l)
    else:
        flat_r = jnp.concatenate([a.reshape(-1) for a in arrays_r])
        flat_l = jnp.concatenate([a.reshape(-1) for a in arrays_l])
    got_l, got_r = recv(flat_r, steps, cyclic), recv(flat_l, -steps, cyclic)

    def split(flat):
        out, at = [], 0
        for shape in shapes:
            if stacked:
                out.append(flat[at:at + shape[0]])
                at += shape[0]
            else:
                size = math.prod(shape)
                out.append(flat[at:at + size].reshape(shape))
                at += size
        return out

    return split(got_l), split(got_r)


def pair_matrix(extent):
    rows = jnp.arange(extent, dtype=jnp.int32)[:, None] // 2
    cols = jnp.arange(extent // 2, dtype=jnp.int32)[None, :]
    return (rows == cols).astype(jnp.float32)


def shrink_sides(field):
    extent_y = field.shape[1]
    extent_z = field.shape[2]
    along_z = jnp.einsum("xyz,zw->xyw", field, pair_matrix(extent_z), precision=EXACT)
    return jnp.einsum("xyw,yv->xvw", along_z, pair_matrix(extent_y), precision=EXACT)


def grow_sides(field):
    extent_y = field.shape[1]
    extent_z = field.shape[2]
    along_z = jnp.einsum("xyw,zw->xyz", field, pair_matrix(2 * extent_z), precision=EXACT)
    return jnp.einsum("xvz,yv->xyz", along_z, pair_matrix(2 * extent_y), precision=EXACT)


def coarsen(field):
    extent_x, extent_y, extent_z = field.shape
    planes = field.reshape(extent_x // 2, 2, extent_y, extent_z).sum(axis=1)
    return shrink_sides(planes) * 0.125


def refine(field):
    extent_x, extent_y, extent_z = field.shape
    wider = grow_sides(field)
    spread = jnp.broadcast_to(wider[:, None], (extent_x, 2, 2 * extent_y, 2 * extent_z))
    return spread.reshape(2 * extent_x, 2 * extent_y, 2 * extent_z)


def make_coefs(rho_ext, inv_spacing):
    two_s = 2.0 * inv_spacing
    center = rho_ext[1:-1]
    safe = jnp.where(center > 0, center, 1.0)
    padded = jnp.pad(center, ((0, 0), (1, 1), (1, 1)), mode="edge")
    near = [
        rho_ext[:-2],
        rho_ext[2:],
        padded[:, :-2, 1:-1],
        padded[:, 2:, 1:-1],
        padded[:, 1:-1, :-2],
        padded[:, 1:-1, 2:],
    ]
    faces = [two_s / (safe + jnp.where(nb > 0, nb, safe)) for nb in near]
    diag = faces[0] + faces[1] + faces[2] + faces[3] + faces[4] + faces[5]
    lo, hi = rho_ext[:-1], rho_ext[1:]
    kxo = jnp.where((lo > 0) & (hi > 0), two_s / (lo + hi), 0.0)
    return {
        "kxo": kxo,
        "kyl": faces[2],
        "kyh": faces[3],
        "kzl": faces[4],
        "kzh": faces[5],
        "w": OMEGA / diag,
        "diag": diag,
    }


def side_terms(field, co, lo, hi):
    padded = jnp.pad(field, ((0, 0), (1, 1), (1, 1)))
    return (
        co["kyl"][lo:hi] * padded[:, :-2, 1:-1]
        + co["kyh"][lo:hi] * padded[:, 2:, 1:-1]
        + co["kzl"][lo:hi] * padded[:, 1:-1, :-2]
        + co["kzh"][lo:hi] * padded[:, 1:-1, 2:]
    )


def smooth(resid, co, sweeps):
    length = resid.shape[0]
    kxo = co["kxo"][1:-1]
    update = co["w"] * resid
    for sweep_no in range(1, sweeps):
        lo, hi = sweep_no, length - sweep_no
        inner = update[1:-1]
        off = (
            kxo[lo - 1:hi - 1] * update[:-2]
            + kxo[lo:hi] * update[2:]
            + side_terms(inner, co, lo, hi)
        )
        update = (1.0 - OMEGA) * inner + co["w"][lo:hi] * (resid[lo:hi] + off)
    return update


ROWS = 64
PAD = 8
VMEM_LIMIT = 64 * 1024 * 1024


def _zero_pads(buf):
    extent_y, extent_z = buf.shape[1] - 2 * PAD, buf.shape[2]
    zeros = jnp.zeros((PAD, extent_z), jnp.float32)

    def body(p, carry):
        buf[p, pl.ds(0, PAD), :] = zeros
        buf[p, pl.ds(PAD + extent_y, PAD), :] = zeros
        return carry

    lax.fori_loop(0, buf.shape[0], body, 0)


def _plane_loop(first, last, extent_y, body):
    def step(i, carry):
        for y0 in range(0, extent_y, ROWS):
            body(first + i, y0)
        return carry

    lax.fori_loop(0, last - first, step, 0)


def _neighbour_sum(src, at, y0, kxo_lo, kxo_hi, kyl, kyh, kzl, kzh):
    extent_z = src.shape[2]
    center = src[at, pl.ds(PAD + y0, ROWS), :]
    below = src[at, pl.ds(PAD + y0 - 1, ROWS), :]
    above = src[at, pl.ds(PAD + y0 + 1, ROWS), :]
    left = pltpu.roll(center, 1, 1)
    right = pltpu.roll(center, extent_z - 1, 1)
    off = (
        kxo_lo * src[at - 1, pl.ds(PAD + y0, ROWS), :]
        + kxo_hi * src[at + 1, pl.ds(PAD + y0, ROWS), :]
        + kyl * below
        + kyh * above
        + kzl * left
        + kzh * right
    )
    return center, off


def _smooth_in_vmem(resid, kxo, kyl, kyh, kzl, kzh, w, out, bufs, sweeps):
    length, extent_y = resid.shape[0], resid.shape[1]
    for buf in bufs:
        _zero_pads(buf)

    def first(q, y0):
        rows = pl.ds(y0, ROWS)
        bufs[0][q, pl.ds(PAD + y0, ROWS), :] = w[q, rows, :] * resid[q, rows, :]

    _plane_loop(0, length, extent_y, first)
    for sweep_no in range(1, sweeps):
        src = bufs[(sweep_no - 1) % 2]
        src_at = sweep_no - 1
        last = sweep_no == sweeps - 1
        dst = out if last else bufs[sweep_no % 2]
        dst_at = sweep_no

        def body(q, y0, src=src, src_at=src_at, dst=dst, dst_at=dst_at, last=last):
            rows = pl.ds(y0, ROWS)
            center, off = _neighbour_sum(
                src, q - src_at, y0, kxo[q - 1, rows, :], kxo[q, rows, :],
                kyl[q, rows, :], kyh[q, rows, :], kzl[q, rows, :], kzh[q, rows, :],
            )
            new = (1.0 - OMEGA) * center + w[q, rows, :] * (resid[q, rows, :] + off)
            if last:
                dst[q - dst_at, rows, :] = new
            else:
                dst[q - dst_at, pl.ds(PAD + y0, ROWS), :] = new

        _plane_loop(sweep_no, length - sweep_no, extent_y, body)


def _fine_first_kernel(resid, kxo, kyl, kyh, kzl, kzh, w, out, buf_a, buf_b):
    _smooth_in_vmem(resid, kxo, kyl, kyh, kzl, kzh, w, out, (buf_a, buf_b), SWEEPS)


def _fine_second_kernel(
    fine_ext, rhs, kxo_full, kyl, kyh, kzl, kzh, w, diag, out, resid_out, held, resid, buf_a, buf_b
):
    planes, extent_y = fine_ext.shape[0], fine_ext.shape[1]
    _zero_pads(held)

    def copy_in(q, y0):
        held[q, pl.ds(PAD + y0, ROWS), :] = fine_ext[q, pl.ds(y0, ROWS), :]

    _plane_loop(0, planes, extent_y, copy_in)

    def residual(q, y0):
        rows = pl.ds(y0, ROWS)
        center, off = _neighbour_sum(
            held, q + 1, y0, kxo_full[q, rows, :], kxo_full[q + 1, rows, :],
            kyl[q, rows, :], kyh[q, rows, :], kzl[q, rows, :], kzh[q, rows, :],
        )
        resid[q, rows, :] = rhs[q, rows, :] - (diag[q, rows, :] * center - off)

    _plane_loop(0, planes - 2, extent_y, residual)
    ghosts = SWEEPS - 1

    def copy_out(q, y0):
        rows = pl.ds(y0, ROWS)
        resid_out[q - ghosts, rows, :] = resid[q, rows, :]

    _plane_loop(ghosts, planes - 2 - ghosts, extent_y, copy_out)
    _smooth_in_vmem(
        resid, kxo_full.at[1:-1], kyl, kyh, kzl, kzh, w, out, (buf_a, buf_b), SWEEPS
    )


def _vmem_call(kernel, outs, scratch, *args):
    return pl.pallas_call(
        kernel,
        out_shape=outs,
        in_specs=[pl.BlockSpec(memory_space=pltpu.VMEM)] * len(args),
        out_specs=(
            [pl.BlockSpec(memory_space=pltpu.VMEM)] * len(outs)
            if isinstance(outs, (list, tuple))
            else pl.BlockSpec(memory_space=pltpu.VMEM)
        ),
        scratch_shapes=scratch,
        compiler_params=pltpu.CompilerParams(vmem_limit_bytes=VMEM_LIMIT),
    )(*args)


def fine_coefs(co):
    extent_y, extent_z = co["kyl"].shape[1], co["kyl"].shape[2]
    ys = jnp.arange(extent_y, dtype=jnp.int32)[None, :, None]
    zs = jnp.arange(extent_z, dtype=jnp.int32)[None, None, :]
    return {
        "kyl": jnp.where(ys == 0, 0.0, co["kyl"]),
        "kyh": jnp.where(ys == extent_y - 1, 0.0, co["kyh"]),
        "kzl": jnp.where(zs == 0, 0.0, co["kzl"]),
        "kzh": jnp.where(zs == extent_z - 1, 0.0, co["kzh"]),
    }


def fine_smooth(resid_ext, co, fc):
    length, extent_y, extent_z = resid_ext.shape
    out = jax.ShapeDtypeStruct((length - 2 * (SWEEPS - 1), extent_y, extent_z), jnp.float32)
    padded = lambda planes: pltpu.VMEM((planes, extent_y + 2 * PAD, extent_z), jnp.float32)
    return _vmem_call(
        _fine_first_kernel, out, [padded(length), padded(length - 2)],
        resid_ext, co["kxo"][1:-1], fc["kyl"], fc["kyh"], fc["kzl"], fc["kzh"], co["w"],
    )


def fine_second(fine_ext, rhs_ext, co, fc):
    planes, extent_y, extent_z = fine_ext.shape
    length = planes - 2
    block = length - 2 * (SWEEPS - 1)
    outs = [jax.ShapeDtypeStruct((block, extent_y, extent_z), jnp.float32)] * 2
    padded = lambda n: pltpu.VMEM((n, extent_y + 2 * PAD, extent_z), jnp.float32)
    return _vmem_call(
        _fine_second_kernel, outs,
        [padded(planes), pltpu.VMEM((length, extent_y, extent_z), jnp.float32),
         padded(length), padded(length - 2)],
        fine_ext, rhs_ext, co["kxo"], fc["kyl"], fc["kyh"], fc["kzl"], fc["kzh"], co["w"], co["diag"],
    )


def per_device(right_side, density):
    me = lax.axis_index("gx")

    (dl, rl), (dr, rr) = exchange(
        [density[-3:], right_side[-2:]], [density[:3], right_side[:2]], 1
    )
    rho0_ext = jnp.concatenate([dl, density, dr])
    rhs_ext = jnp.concatenate([rl, right_side, rr])
    co0 = make_coefs(rho0_ext, 1.0)

    rho1 = coarsen(density)
    rho2 = coarsen(rho1)
    rho3 = coarsen(rho2)

    def restrict(resid):
        r1 = coarsen(resid)
        r2 = coarsen(r1)
        return r1, r2, coarsen(r2)

    def gather_coarse(r1, r2, r3, with_rho):
        to_right = [r1[-2:], r2, r3]
        to_left = [r1[:2], r2, r3]
        if with_rho:
            to_right += [rho1[-3:], rho2, rho3]
            to_left += [rho1[:3], rho2, rho3]
        got_l, got_r = exchange(to_right, to_left, 1, True)
        r1e = jnp.concatenate([got_l[0], r1, got_r[0]])
        r2e = jnp.concatenate([got_l[1], r2, got_r[1]])
        win3 = [jnp.concatenate([got_l[2], r3, got_r[2]])]
        extra = {}
        if with_rho:
            extra["rho1e"] = jnp.concatenate([got_l[3], rho1, got_r[3]])
            rho2_l, rho2_r = got_l[4], got_r[4]
            win3.append(jnp.concatenate([got_l[5], rho3, got_r[5]]))
        to_right = list(win3)
        to_left = list(win3)
        if with_rho:
            to_right.append(rho2_r[-1:])
            to_left.append(rho2_l[:1])
        got_l, got_r = exchange(to_right, to_left, 3, True)
        win9 = [jnp.concatenate([got_l[k], win3[k], got_r[k]]) for k in range(len(win3))]
        if with_rho:
            extra["rho2e"] = jnp.concatenate([got_l[-1], rho2_l, rho2, rho2_r, got_r[-1]])
        got_l, got_r = exchange(win9, win9, 9, True)
        win27 = [jnp.concatenate([got_l[k], win9[k], got_r[k]]) for k in range(len(win9))]
        win27 = [part * inside(1, 13, 27) for part in win27]
        r1e = r1e * inside(4, 2, r1e.shape[0])
        r2e = r2e * inside(2, 2, r2e.shape[0])
        if with_rho:
            extra["rho1e"] = extra["rho1e"] * inside(4, 3, extra["rho1e"].shape[0])
            extra["rho2e"] = extra["rho2e"] * inside(2, 3, extra["rho2e"].shape[0])
        return r1e, r2e, win27, extra

    r1, r2, r3 = restrict(right_side)
    r1e, r2e, win, extra = gather_coarse(r1, r2, r3, True)
    r3w, rho3w = win
    co1 = make_coefs(extra["rho1e"], 0.25)
    co2 = make_coefs(extra["rho2e"], 0.25**2)
    center = 13
    co3 = make_coefs(rho3w[center - 3:center + 4], 0.25**3)
    pair_start = 1 - me % 2

    def to_top(window):
        return coarsen(lax.dynamic_slice_in_dim(window, pair_start, 2 * center))

    co4 = make_coefs(to_top(rho3w), 0.25**4)

    def coarse_part(r1e, r2e, r3w):
        top = smooth(to_top(r3w)[1:-1], co4, TOP_SWEEPS)
        summed = grow_sides(top) + smooth(r3w[center - 2:center + 3], co3, SWEEPS)
        summed = refine(summed) + smooth(r2e, co2, SWEEPS)
        summed = refine(summed) + smooth(r1e, co1, SWEEPS)
        return refine(summed)

    fc0 = fine_coefs(co0)
    fine_0 = fine_smooth(rhs_ext, co0, fc0)
    coarse_0 = coarse_part(r1e, r2e, r3w)

    (fl,), (fr,) = exchange([fine_0[-3:]], [fine_0[:3]], 1)
    fine_ext = jnp.concatenate([fl, fine_0, fr])
    fine_1, resid_block = fine_second(fine_ext, rhs_ext, co0, fc0)
    r1, r2, r3 = restrict(resid_block)
    r1e, r2e, win, _ = gather_coarse(r1, r2, r3, False)
    coarse_1 = coarse_part(r1e, r2e, win[0])

    pressure = (fine_0 + fine_1) + coarse_0
    return (pressure, coarse_1)


def solution(mesh):
    return jax.shard_map(
        per_device,
        mesh=mesh,
        in_specs=(P("gx", None, None), P("gx", None, None)),
        out_specs=(P("gx", None, None), P("gx", None, None)),
        check_vma=False,
    )
```

```python
import math

import jax
import jax.numpy as jnp
from jax import lax
from jax.experimental import pallas as pl
from jax.experimental.pallas import tpu as pltpu
from jax.sharding import PartitionSpec as P

SWEEPS = 3
TOP_SWEEPS = 6
CYCLES = 2


OMEGA = 0.8
EXACT = lax.Precision.HIGHEST


def recv(value, steps, cyclic):
    count = lax.axis_size("gx")
    if cyclic:
        pairs = [(i, (i + steps) % count) for i in range(count)]
    else:
        pairs = [(i, i + steps) for i in range(count) if 0 <= i + steps < count]
    return lax.ppermute(value, "gx", pairs)


def inside(per_device, ghosts, length):
    count = lax.axis_size("gx")
    first = lax.axis_index("gx") * per_device - ghosts
    index = first + jnp.arange(length, dtype=jnp.int32)
    keep = (index >= 0) & (index < count * per_device)
    return keep.astype(jnp.float32)[:, None, None]


def exchange(to_right, to_left, steps, cyclic=False):
    arrays_r, arrays_l = list(to_right), list(to_left)
    shapes = [a.shape for a in arrays_r]
    stacked = all(shape[1:] == shapes[0][1:] for shape in shapes)
    if stacked:
        flat_r = jnp.concatenate(arrays_r)
        flat_l = jnp.concatenate(arrays_l)
    else:
        flat_r = jnp.concatenate([a.reshape(-1) for a in arrays_r])
        flat_l = jnp.concatenate([a.reshape(-1) for a in arrays_l])
    got_l, got_r = recv(flat_r, steps, cyclic), recv(flat_l, -steps, cyclic)

    def split(flat):
        out, at = [], 0
        for shape in shapes:
            if stacked:
                out.append(flat[at:at + shape[0]])
                at += shape[0]
            else:
                size = math.prod(shape)
                out.append(flat[at:at + size].reshape(shape))
                at += size
        return out

    return split(got_l), split(got_r)


def pair_matrix(extent):
    rows = jnp.arange(extent, dtype=jnp.int32)[:, None] // 2
    cols = jnp.arange(extent // 2, dtype=jnp.int32)[None, :]
    return (rows == cols).astype(jnp.float32)


def shrink_sides(field):
    extent_y = field.shape[1]
    extent_z = field.shape[2]
    along_z = jnp.einsum("xyz,zw->xyw", field, pair_matrix(extent_z), precision=EXACT)
    return jnp.einsum("xyw,yv->xvw", along_z, pair_matrix(extent_y), precision=EXACT)


def grow_sides(field):
    extent_y = field.shape[1]
    extent_z = field.shape[2]
    along_z = jnp.einsum("xyw,zw->xyz", field, pair_matrix(2 * extent_z), precision=EXACT)
    return jnp.einsum("xvz,yv->xyz", along_z, pair_matrix(2 * extent_y), precision=EXACT)


def coarsen(field):
    extent_x, extent_y, extent_z = field.shape
    planes = field.reshape(extent_x // 2, 2, extent_y, extent_z).sum(axis=1)
    return shrink_sides(planes) * 0.125


def refine(field):
    extent_x, extent_y, extent_z = field.shape
    wider = grow_sides(field)
    spread = jnp.broadcast_to(wider[:, None], (extent_x, 2, 2 * extent_y, 2 * extent_z))
    return spread.reshape(2 * extent_x, 2 * extent_y, 2 * extent_z)


def make_coefs(rho_ext, inv_spacing, zero_sides=False):
    two_s = 2.0 * inv_spacing
    center = rho_ext[1:-1]
    safe = jnp.where(center > 0, center, 1.0)
    padded = jnp.pad(center, ((0, 0), (1, 1), (1, 1)), mode="edge")
    near = [
        rho_ext[:-2],
        rho_ext[2:],
        padded[:, :-2, 1:-1],
        padded[:, 2:, 1:-1],
        padded[:, 1:-1, :-2],
        padded[:, 1:-1, 2:],
    ]
    faces = [two_s / (safe + jnp.where(nb > 0, nb, safe)) for nb in near]
    diag = faces[0] + faces[1] + faces[2] + faces[3] + faces[4] + faces[5]
    sides = faces[2:]
    if zero_sides:
        extent_y, extent_z = center.shape[1], center.shape[2]
        ys = jnp.arange(extent_y, dtype=jnp.int32)[None, :, None]
        zs = jnp.arange(extent_z, dtype=jnp.int32)[None, None, :]
        sides = [
            jnp.where(ys == 0, 0.0, sides[0]),
            jnp.where(ys == extent_y - 1, 0.0, sides[1]),
            jnp.where(zs == 0, 0.0, sides[2]),
            jnp.where(zs == extent_z - 1, 0.0, sides[3]),
        ]
    lo, hi = rho_ext[:-1], rho_ext[1:]
    kxo = jnp.where((lo > 0) & (hi > 0), two_s / (lo + hi), 0.0)
    return {
        "kxo": kxo,
        "kyl": sides[0],
        "kyh": sides[1],
        "kzl": sides[2],
        "kzh": sides[3],
        "w": OMEGA / diag,
        "diag": diag,
    }


def side_terms(field, co, lo, hi):
    padded = jnp.pad(field, ((0, 0), (1, 1), (1, 1)))
    return (
        co["kyl"][lo:hi] * padded[:, :-2, 1:-1]
        + co["kyh"][lo:hi] * padded[:, 2:, 1:-1]
        + co["kzl"][lo:hi] * padded[:, 1:-1, :-2]
        + co["kzh"][lo:hi] * padded[:, 1:-1, 2:]
    )


def smooth(resid, co, sweeps):
    length = resid.shape[0]
    kxo = co["kxo"][1:-1]
    update = co["w"] * resid
    for sweep_no in range(1, sweeps):
        lo, hi = sweep_no, length - sweep_no
        inner = update[1:-1]
        off = (
            kxo[lo - 1:hi - 1] * update[:-2]
            + kxo[lo:hi] * update[2:]
            + side_terms(inner, co, lo, hi)
        )
        update = (1.0 - OMEGA) * inner + co["w"][lo:hi] * (resid[lo:hi] + off)
    return update


ROWS = 64
PAD = 8
VMEM_LIMIT = 64 * 1024 * 1024


def _zero_pads(buf):
    extent_y, extent_z = buf.shape[1] - 2 * PAD, buf.shape[2]
    zeros = jnp.zeros((PAD, extent_z), jnp.float32)

    def body(p, carry):
        buf[p, pl.ds(0, PAD), :] = zeros
        buf[p, pl.ds(PAD + extent_y, PAD), :] = zeros
        return carry

    lax.fori_loop(0, buf.shape[0], body, 0)


def _plane_loop(first, last, extent_y, body):
    def step(i, carry):
        for y0 in range(0, extent_y, ROWS):
            body(first + i, y0)
        return carry

    lax.fori_loop(0, last - first, step, 0)


def _neighbour_sum(src, at, y0, kxo_lo, kxo_hi, kyl, kyh, kzl, kzh):
    extent_z = src.shape[2]
    center = src[at, pl.ds(PAD + y0, ROWS), :]
    below = src[at, pl.ds(PAD + y0 - 1, ROWS), :]
    above = src[at, pl.ds(PAD + y0 + 1, ROWS), :]
    left = pltpu.roll(center, 1, 1)
    right = pltpu.roll(center, extent_z - 1, 1)
    off = (
        kxo_lo * src[at - 1, pl.ds(PAD + y0, ROWS), :]
        + kxo_hi * src[at + 1, pl.ds(PAD + y0, ROWS), :]
        + kyl * below
        + kyh * above
        + kzl * left
        + kzh * right
    )
    return center, off


def _smooth_in_vmem(resid, kxo, kyl, kyh, kzl, kzh, w, out, bufs, sweeps):
    length, extent_y = resid.shape[0], resid.shape[1]
    for buf in bufs:
        _zero_pads(buf)

    def first(q, y0):
        rows = pl.ds(y0, ROWS)
        bufs[0][q, pl.ds(PAD + y0, ROWS), :] = w[q, rows, :] * resid[q, rows, :]

    _plane_loop(0, length, extent_y, first)
    for sweep_no in range(1, sweeps):
        src = bufs[(sweep_no - 1) % 2]
        src_at = sweep_no - 1
        last = sweep_no == sweeps - 1
        dst = out if last else bufs[sweep_no % 2]
        dst_at = sweep_no

        def body(q, y0, src=src, src_at=src_at, dst=dst, dst_at=dst_at, last=last):
            rows = pl.ds(y0, ROWS)
            center, off = _neighbour_sum(
                src, q - src_at, y0, kxo[q - 1, rows, :], kxo[q, rows, :],
                kyl[q, rows, :], kyh[q, rows, :], kzl[q, rows, :], kzh[q, rows, :],
            )
            new = (1.0 - OMEGA) * center + w[q, rows, :] * (resid[q, rows, :] + off)
            if last:
                dst[q - dst_at, rows, :] = new
            else:
                dst[q - dst_at, pl.ds(PAD + y0, ROWS), :] = new

        _plane_loop(sweep_no, length - sweep_no, extent_y, body)


def _fine_first_kernel(resid, kxo, kyl, kyh, kzl, kzh, w, out, buf_a, buf_b):
    _smooth_in_vmem(resid, kxo, kyl, kyh, kzl, kzh, w, out, (buf_a, buf_b), SWEEPS)


def _fine_second_kernel(
    fine_ext, rhs, kxo_full, kyl, kyh, kzl, kzh, w, diag, out, resid_out, held, resid, buf_a, buf_b
):
    planes, extent_y = fine_ext.shape[0], fine_ext.shape[1]
    _zero_pads(held)

    def copy_in(q, y0):
        held[q, pl.ds(PAD + y0, ROWS), :] = fine_ext[q, pl.ds(y0, ROWS), :]

    _plane_loop(0, planes, extent_y, copy_in)

    def residual(q, y0):
        rows = pl.ds(y0, ROWS)
        center, off = _neighbour_sum(
            held, q + 1, y0, kxo_full[q, rows, :], kxo_full[q + 1, rows, :],
            kyl[q, rows, :], kyh[q, rows, :], kzl[q, rows, :], kzh[q, rows, :],
        )
        resid[q, rows, :] = rhs[q, rows, :] - (diag[q, rows, :] * center - off)

    _plane_loop(0, planes - 2, extent_y, residual)
    ghosts = SWEEPS - 1

    def copy_out(q, y0):
        rows = pl.ds(y0, ROWS)
        resid_out[q - ghosts, rows, :] = resid[q, rows, :]

    _plane_loop(ghosts, planes - 2 - ghosts, extent_y, copy_out)
    _smooth_in_vmem(
        resid, kxo_full.at[1:-1], kyl, kyh, kzl, kzh, w, out, (buf_a, buf_b), SWEEPS
    )


def _vmem_call(kernel, outs, scratch, *args):
    return pl.pallas_call(
        kernel,
        out_shape=outs,
        in_specs=[pl.BlockSpec(memory_space=pltpu.VMEM)] * len(args),
        out_specs=(
            [pl.BlockSpec(memory_space=pltpu.VMEM)] * len(outs)
            if isinstance(outs, (list, tuple))
            else pl.BlockSpec(memory_space=pltpu.VMEM)
        ),
        scratch_shapes=scratch,
        compiler_params=pltpu.CompilerParams(vmem_limit_bytes=VMEM_LIMIT),
    )(*args)


def fine_smooth(resid_ext, co):
    length, extent_y, extent_z = resid_ext.shape
    out = jax.ShapeDtypeStruct((length - 2 * (SWEEPS - 1), extent_y, extent_z), jnp.float32)
    padded = lambda planes: pltpu.VMEM((planes, extent_y + 2 * PAD, extent_z), jnp.float32)
    return _vmem_call(
        _fine_first_kernel, out, [padded(length), padded(length - 2)],
        resid_ext, co["kxo"][1:-1], co["kyl"], co["kyh"], co["kzl"], co["kzh"], co["w"],
    )


def fine_second(fine_ext, rhs_ext, co):
    planes, extent_y, extent_z = fine_ext.shape
    length = planes - 2
    block = length - 2 * (SWEEPS - 1)
    outs = [jax.ShapeDtypeStruct((block, extent_y, extent_z), jnp.float32)] * 2
    padded = lambda n: pltpu.VMEM((n, extent_y + 2 * PAD, extent_z), jnp.float32)
    return _vmem_call(
        _fine_second_kernel, outs,
        [padded(planes), pltpu.VMEM((length, extent_y, extent_z), jnp.float32),
         padded(length), padded(length - 2)],
        fine_ext, rhs_ext, co["kxo"], co["kyl"], co["kyh"], co["kzl"], co["kzh"], co["w"], co["diag"],
    )


def per_device(right_side, density):
    me = lax.axis_index("gx")

    (dl, rl), (dr, rr) = exchange(
        [density[-3:], right_side[-2:]], [density[:3], right_side[:2]], 1
    )
    rho0_ext = jnp.concatenate([dl, density, dr])
    rhs_ext = jnp.concatenate([rl, right_side, rr])
    co0 = make_coefs(rho0_ext, 1.0, zero_sides=True)

    fine_0 = fine_smooth(rhs_ext, co0)

    (fl,), (fr,) = exchange([fine_0[-3:]], [fine_0[:3]], 1)
    fine_ext = jnp.concatenate([fl, fine_0, fr])
    fine_1, resid_block = fine_second(fine_ext, rhs_ext, co0)

    rho1 = coarsen(density)
    rho2 = coarsen(rho1)
    rho3 = coarsen(rho2)

    def restrict(resid):
        r1 = coarsen(resid)
        r2 = coarsen(r1)
        return r1, r2, coarsen(r2)

    cycles = [restrict(right_side), restrict(resid_block)]
    to_right, to_left = [], []
    for r1, r2, _ in cycles:
        to_right += [r1[-2:], r2]
        to_left += [r1[:2], r2]
    to_right += [rho1[-3:], rho2]
    to_left += [rho1[:3], rho2]
    level3 = jnp.concatenate([r3 for _, _, r3 in cycles] + [rho3])
    to_right.append(level3)
    to_left.append(level3)
    got_l, got_r = exchange(to_right, to_left, 1, True)
    parts = []
    for k, (r1, r2, _) in enumerate(cycles):
        r1e = jnp.concatenate([got_l[2 * k], r1, got_r[2 * k]])
        r2e = jnp.concatenate([got_l[2 * k + 1], r2, got_r[2 * k + 1]])
        parts.append((r1e * inside(4, 2, r1e.shape[0]), r2e * inside(2, 2, r2e.shape[0])))
    at = 2 * len(cycles)
    rho1e = jnp.concatenate([got_l[at], rho1, got_r[at]])
    rho2_l, rho2_r = got_l[at + 1], got_r[at + 1]
    win3 = jnp.concatenate([got_l[-1], level3, got_r[-1]])
    got_l, got_r = exchange([win3, rho2_r[-1:]], [win3, rho2_l[:1]], 3, True)
    win9 = jnp.concatenate([got_l[0], win3, got_r[0]])
    rho2e = jnp.concatenate([got_l[1], rho2_l, rho2, rho2_r, got_r[1]])
    (got_l,), (got_r,) = exchange([win9], [win9], 9, True)
    win27 = jnp.concatenate([got_l, win9, got_r])
    per = len(cycles) + 1
    win27 = win27.reshape(27, per, win27.shape[1], win27.shape[2]) * inside(1, 13, 27)[:, None]
    windows = [win27[:, k] for k in range(per)]
    rho3w = windows[-1]

    co1 = make_coefs(rho1e * inside(4, 3, rho1e.shape[0]), 0.25)
    co2 = make_coefs(rho2e * inside(2, 3, rho2e.shape[0]), 0.25**2)
    center = 13
    co3 = make_coefs(rho3w[center - 3:center + 4], 0.25**3)
    pair_start = 1 - me % 2

    def to_top(window):
        return coarsen(lax.dynamic_slice_in_dim(window, pair_start, 2 * center))

    co4 = make_coefs(to_top(rho3w), 0.25**4)

    def coarse_part(r1e, r2e, r3w):
        top = smooth(to_top(r3w)[1:-1], co4, TOP_SWEEPS)
        summed = grow_sides(top) + smooth(r3w[center - 2:center + 3], co3, SWEEPS)
        summed = refine(summed) + smooth(r2e, co2, SWEEPS)
        summed = refine(summed) + smooth(r1e, co1, SWEEPS)
        return refine(summed)

    coarse_0 = coarse_part(parts[0][0], parts[0][1], windows[0])
    coarse_1 = coarse_part(parts[1][0], parts[1][1], windows[1])
    pressure = (fine_0 + fine_1) + coarse_0
    return (pressure, coarse_1)


def solution(mesh):
    return jax.shard_map(
        per_device,
        mesh=mesh,
        in_specs=(P("gx", None, None), P("gx", None, None)),
        out_specs=(P("gx", None, None), P("gx", None, None)),
        check_vma=False,
    )
```

```python
import math

import jax
import jax.numpy as jnp
from jax import lax
from jax.experimental import pallas as pl
from jax.experimental.pallas import tpu as pltpu
from jax.sharding import PartitionSpec as P

SWEEPS = 3
TOP_SWEEPS = 6
CYCLES = 2


OMEGA = 0.8
EXACT = lax.Precision.HIGHEST


def recv(value, steps, cyclic):
    count = lax.axis_size("gx")
    if cyclic:
        pairs = [(i, (i + steps) % count) for i in range(count)]
    else:
        pairs = [(i, i + steps) for i in range(count) if 0 <= i + steps < count]
    return lax.ppermute(value, "gx", pairs)


def inside(per_device, ghosts, length):
    count = lax.axis_size("gx")
    first = lax.axis_index("gx") * per_device - ghosts
    index = first + jnp.arange(length, dtype=jnp.int32)
    keep = (index >= 0) & (index < count * per_device)
    return keep.astype(jnp.float32)[:, None, None]


def exchange(to_right, to_left, steps, cyclic=False):
    arrays_r, arrays_l = list(to_right), list(to_left)
    shapes = [a.shape for a in arrays_r]
    stacked = all(shape[1:] == shapes[0][1:] for shape in shapes)
    if stacked:
        flat_r = jnp.concatenate(arrays_r)
        flat_l = jnp.concatenate(arrays_l)
    else:
        flat_r = jnp.concatenate([a.reshape(-1) for a in arrays_r])
        flat_l = jnp.concatenate([a.reshape(-1) for a in arrays_l])
    got_l, got_r = recv(flat_r, steps, cyclic), recv(flat_l, -steps, cyclic)

    def split(flat):
        out, at = [], 0
        for shape in shapes:
            if stacked:
                out.append(flat[at:at + shape[0]])
                at += shape[0]
            else:
                size = math.prod(shape)
                out.append(flat[at:at + size].reshape(shape))
                at += size
        return out

    return split(got_l), split(got_r)


def pair_matrix(extent):
    rows = jnp.arange(extent, dtype=jnp.int32)[:, None] // 2
    cols = jnp.arange(extent // 2, dtype=jnp.int32)[None, :]
    return (rows == cols).astype(jnp.float32)


def shrink_sides(field):
    extent_y = field.shape[1]
    extent_z = field.shape[2]
    along_z = jnp.einsum("xyz,zw->xyw", field, pair_matrix(extent_z), precision=EXACT)
    return jnp.einsum("xyw,yv->xvw", along_z, pair_matrix(extent_y), precision=EXACT)


def grow_sides(field):
    extent_y = field.shape[1]
    extent_z = field.shape[2]
    along_z = jnp.einsum("xyw,zw->xyz", field, pair_matrix(2 * extent_z), precision=EXACT)
    return jnp.einsum("xvz,yv->xyz", along_z, pair_matrix(2 * extent_y), precision=EXACT)


def coarsen(field):
    extent_x, extent_y, extent_z = field.shape
    planes = field.reshape(extent_x // 2, 2, extent_y, extent_z).sum(axis=1)
    return shrink_sides(planes) * 0.125


def refine(field):
    extent_x, extent_y, extent_z = field.shape
    wider = grow_sides(field)
    spread = jnp.broadcast_to(wider[:, None], (extent_x, 2, 2 * extent_y, 2 * extent_z))
    return spread.reshape(2 * extent_x, 2 * extent_y, 2 * extent_z)


def make_coefs(rho_ext, inv_spacing):
    two_s = 2.0 * inv_spacing
    center = rho_ext[1:-1]
    safe = jnp.where(center > 0, center, 1.0)
    padded = jnp.pad(center, ((0, 0), (1, 1), (1, 1)), mode="edge")
    near = [
        rho_ext[:-2],
        rho_ext[2:],
        padded[:, :-2, 1:-1],
        padded[:, 2:, 1:-1],
        padded[:, 1:-1, :-2],
        padded[:, 1:-1, 2:],
    ]
    faces = [two_s / (safe + jnp.where(nb > 0, nb, safe)) for nb in near]
    diag = faces[0] + faces[1] + faces[2] + faces[3] + faces[4] + faces[5]
    sides = faces[2:]
    lo, hi = rho_ext[:-1], rho_ext[1:]
    kxo = jnp.where((lo > 0) & (hi > 0), two_s / (lo + hi), 0.0)
    return {
        "kxo": kxo,
        "kyl": sides[0],
        "kyh": sides[1],
        "kzl": sides[2],
        "kzh": sides[3],
        "w": OMEGA / diag,
        "diag": diag,
    }


def side_terms(field, co, lo, hi):
    padded = jnp.pad(field, ((0, 0), (1, 1), (1, 1)))
    return (
        co["kyl"][lo:hi] * padded[:, :-2, 1:-1]
        + co["kyh"][lo:hi] * padded[:, 2:, 1:-1]
        + co["kzl"][lo:hi] * padded[:, 1:-1, :-2]
        + co["kzh"][lo:hi] * padded[:, 1:-1, 2:]
    )


def smooth(resid, co, sweeps):
    length = resid.shape[0]
    kxo = co["kxo"][1:-1]
    update = co["w"] * resid
    for sweep_no in range(1, sweeps):
        lo, hi = sweep_no, length - sweep_no
        inner = update[1:-1]
        off = (
            kxo[lo - 1:hi - 1] * update[:-2]
            + kxo[lo:hi] * update[2:]
            + side_terms(inner, co, lo, hi)
        )
        update = (1.0 - OMEGA) * inner + co["w"][lo:hi] * (resid[lo:hi] + off)
    return update


ROWS = 64
PAD = 8
VMEM_LIMIT = 64 * 1024 * 1024


def _zero_pads(buf):
    extent_y, extent_z = buf.shape[1] - 2 * PAD, buf.shape[2]
    zeros = jnp.zeros((PAD, extent_z), jnp.float32)

    def body(p, carry):
        buf[p, pl.ds(0, PAD), :] = zeros
        buf[p, pl.ds(PAD + extent_y, PAD), :] = zeros
        return carry

    lax.fori_loop(0, buf.shape[0], body, 0)


def _plane_loop(first, last, extent_y, body):
    def step(i, carry):
        for y0 in range(0, extent_y, ROWS):
            body(first + i, y0)
        return carry

    lax.fori_loop(0, last - first, step, 0)


def _neighbour_sum(src, at, y0, kxo_lo, kxo_hi, kyl, kyh, kzl, kzh):
    extent_z = src.shape[2]
    center = src[at, pl.ds(PAD + y0, ROWS), :]
    below = src[at, pl.ds(PAD + y0 - 1, ROWS), :]
    above = src[at, pl.ds(PAD + y0 + 1, ROWS), :]
    lanes = lax.broadcasted_iota(jnp.int32, center.shape, 1)
    left = jnp.where(lanes == 0, 0.0, pltpu.roll(center, 1, 1))
    right = jnp.where(lanes == extent_z - 1, 0.0, pltpu.roll(center, extent_z - 1, 1))
    off = (
        kxo_lo * src[at - 1, pl.ds(PAD + y0, ROWS), :]
        + kxo_hi * src[at + 1, pl.ds(PAD + y0, ROWS), :]
        + kyl * below
        + kyh * above
        + kzl * left
        + kzh * right
    )
    return center, off


def _smooth_in_vmem(resid, kxo, kyl, kyh, kzl, kzh, w, out, bufs, sweeps):
    length, extent_y = resid.shape[0], resid.shape[1]
    for buf in bufs:
        _zero_pads(buf)

    def first(q, y0):
        rows = pl.ds(y0, ROWS)
        bufs[0][q, pl.ds(PAD + y0, ROWS), :] = w[q, rows, :] * resid[q, rows, :]

    _plane_loop(0, length, extent_y, first)
    for sweep_no in range(1, sweeps):
        src = bufs[(sweep_no - 1) % 2]
        src_at = sweep_no - 1
        last = sweep_no == sweeps - 1
        dst = out if last else bufs[sweep_no % 2]
        dst_at = sweep_no

        def body(q, y0, src=src, src_at=src_at, dst=dst, dst_at=dst_at, last=last):
            rows = pl.ds(y0, ROWS)
            center, off = _neighbour_sum(
                src, q - src_at, y0, kxo[q - 1, rows, :], kxo[q, rows, :],
                kyl[q, rows, :], kyh[q, rows, :], kzl[q, rows, :], kzh[q, rows, :],
            )
            new = (1.0 - OMEGA) * center + w[q, rows, :] * (resid[q, rows, :] + off)
            if last:
                dst[q - dst_at, rows, :] = new
            else:
                dst[q - dst_at, pl.ds(PAD + y0, ROWS), :] = new

        _plane_loop(sweep_no, length - sweep_no, extent_y, body)


def _fine_first_kernel(resid, kxo, kyl, kyh, kzl, kzh, w, out, buf_a, buf_b):
    _smooth_in_vmem(resid, kxo, kyl, kyh, kzl, kzh, w, out, (buf_a, buf_b), SWEEPS)


def _fine_second_kernel(
    fine_ext, rhs, kxo_full, kyl, kyh, kzl, kzh, w, diag, out, resid_out, held, resid, buf_a, buf_b
):
    planes, extent_y = fine_ext.shape[0], fine_ext.shape[1]
    _zero_pads(held)

    def copy_in(q, y0):
        held[q, pl.ds(PAD + y0, ROWS), :] = fine_ext[q, pl.ds(y0, ROWS), :]

    _plane_loop(0, planes, extent_y, copy_in)

    def residual(q, y0):
        rows = pl.ds(y0, ROWS)
        center, off = _neighbour_sum(
            held, q + 1, y0, kxo_full[q, rows, :], kxo_full[q + 1, rows, :],
            kyl[q, rows, :], kyh[q, rows, :], kzl[q, rows, :], kzh[q, rows, :],
        )
        resid[q, rows, :] = rhs[q, rows, :] - (diag[q, rows, :] * center - off)

    _plane_loop(0, planes - 2, extent_y, residual)
    ghosts = SWEEPS - 1

    def copy_out(q, y0):
        rows = pl.ds(y0, ROWS)
        resid_out[q - ghosts, rows, :] = resid[q, rows, :]

    _plane_loop(ghosts, planes - 2 - ghosts, extent_y, copy_out)
    _smooth_in_vmem(
        resid, kxo_full.at[1:-1], kyl, kyh, kzl, kzh, w, out, (buf_a, buf_b), SWEEPS
    )


def _vmem_call(kernel, outs, scratch, *args):
    return pl.pallas_call(
        kernel,
        out_shape=outs,
        in_specs=[pl.BlockSpec(memory_space=pltpu.VMEM)] * len(args),
        out_specs=(
            [pl.BlockSpec(memory_space=pltpu.VMEM)] * len(outs)
            if isinstance(outs, (list, tuple))
            else pl.BlockSpec(memory_space=pltpu.VMEM)
        ),
        scratch_shapes=scratch,
        compiler_params=pltpu.CompilerParams(vmem_limit_bytes=VMEM_LIMIT),
    )(*args)


def fine_smooth(resid_ext, co):
    length, extent_y, extent_z = resid_ext.shape
    out = jax.ShapeDtypeStruct((length - 2 * (SWEEPS - 1), extent_y, extent_z), jnp.float32)
    padded = lambda planes: pltpu.VMEM((planes, extent_y + 2 * PAD, extent_z), jnp.float32)
    return _vmem_call(
        _fine_first_kernel, out, [padded(length), padded(length - 2)],
        resid_ext, co["kxo"][1:-1], co["kyl"], co["kyh"], co["kzl"], co["kzh"], co["w"],
    )


def fine_second(fine_ext, rhs_ext, co):
    planes, extent_y, extent_z = fine_ext.shape
    length = planes - 2
    block = length - 2 * (SWEEPS - 1)
    outs = [jax.ShapeDtypeStruct((block, extent_y, extent_z), jnp.float32)] * 2
    padded = lambda n: pltpu.VMEM((n, extent_y + 2 * PAD, extent_z), jnp.float32)
    return _vmem_call(
        _fine_second_kernel, outs,
        [padded(planes), pltpu.VMEM((length, extent_y, extent_z), jnp.float32),
         padded(length), padded(length - 2)],
        fine_ext, rhs_ext, co["kxo"], co["kyl"], co["kyh"], co["kzl"], co["kzh"], co["w"], co["diag"],
    )


def per_device(right_side, density):
    me = lax.axis_index("gx")

    (dl, rl), (dr, rr) = exchange(
        [density[-3:], right_side[-2:]], [density[:3], right_side[:2]], 1
    )
    rho0_ext = jnp.concatenate([dl, density, dr])
    rhs_ext = jnp.concatenate([rl, right_side, rr])
    co0 = make_coefs(rho0_ext, 1.0)

    fine_0 = fine_smooth(rhs_ext, co0)

    (fl,), (fr,) = exchange([fine_0[-3:]], [fine_0[:3]], 1)
    fine_ext = jnp.concatenate([fl, fine_0, fr])
    fine_1, resid_block = fine_second(fine_ext, rhs_ext, co0)

    rho1 = coarsen(density)
    rho2 = coarsen(rho1)
    rho3 = coarsen(rho2)

    def restrict(resid):
        r1 = coarsen(resid)
        r2 = coarsen(r1)
        return r1, r2, coarsen(r2)

    cycles = [restrict(right_side), restrict(resid_block)]
    to_right, to_left = [], []
    for r1, r2, _ in cycles:
        to_right += [r1[-2:], r2]
        to_left += [r1[:2], r2]
    to_right += [rho1[-3:], rho2]
    to_left += [rho1[:3], rho2]
    level3 = jnp.concatenate([r3 for _, _, r3 in cycles] + [rho3])
    to_right.append(level3)
    to_left.append(level3)
    got_l, got_r = exchange(to_right, to_left, 1, True)
    parts = []
    for k, (r1, r2, _) in enumerate(cycles):
        r1e = jnp.concatenate([got_l[2 * k], r1, got_r[2 * k]])
        r2e = jnp.concatenate([got_l[2 * k + 1], r2, got_r[2 * k + 1]])
        parts.append((r1e * inside(4, 2, r1e.shape[0]), r2e * inside(2, 2, r2e.shape[0])))
    at = 2 * len(cycles)
    rho1e = jnp.concatenate([got_l[at], rho1, got_r[at]])
    rho2_l, rho2_r = got_l[at + 1], got_r[at + 1]
    win3 = jnp.concatenate([got_l[-1], level3, got_r[-1]])
    got_l, got_r = exchange([win3, rho2_r[-1:]], [win3, rho2_l[:1]], 3, True)
    win9 = jnp.concatenate([got_l[0], win3, got_r[0]])
    rho2e = jnp.concatenate([got_l[1], rho2_l, rho2, rho2_r, got_r[1]])
    (got_l,), (got_r,) = exchange([win9], [win9], 9, True)
    win27 = jnp.concatenate([got_l, win9, got_r])
    per = len(cycles) + 1
    win27 = win27.reshape(27, per, win27.shape[1], win27.shape[2]) * inside(1, 13, 27)[:, None]
    windows = [win27[:, k] for k in range(per)]
    rho3w = windows[-1]

    co1 = make_coefs(rho1e * inside(4, 3, rho1e.shape[0]), 0.25)
    co2 = make_coefs(rho2e * inside(2, 3, rho2e.shape[0]), 0.25**2)
    center = 13
    co3 = make_coefs(rho3w[center - 3:center + 4], 0.25**3)
    pair_start = 1 - me % 2

    def to_top(window):
        return coarsen(lax.dynamic_slice_in_dim(window, pair_start, 2 * center))

    co4 = make_coefs(to_top(rho3w), 0.25**4)

    def coarse_part(r1e, r2e, r3w):
        top = smooth(to_top(r3w)[1:-1], co4, TOP_SWEEPS)
        summed = grow_sides(top) + smooth(r3w[center - 2:center + 3], co3, SWEEPS)
        summed = refine(summed) + smooth(r2e, co2, SWEEPS)
        summed = refine(summed) + smooth(r1e, co1, SWEEPS)
        return refine(summed)

    coarse = jax.vmap(coarse_part)(
        jnp.stack([parts[0][0], parts[1][0]]),
        jnp.stack([parts[0][1], parts[1][1]]),
        jnp.stack(windows[:2]),
    )
    pressure = (fine_0 + fine_1) + coarse[0]
    return (pressure, coarse[1])


def solution(mesh):
    return jax.shard_map(
        per_device,
        mesh=mesh,
        in_specs=(P("gx", None, None), P("gx", None, None)),
        out_specs=(P("gx", None, None), P("gx", None, None)),
        check_vma=False,
    )
```

```python
import math

import jax
import jax.numpy as jnp
from jax import lax
from jax.experimental import pallas as pl
from jax.experimental.pallas import tpu as pltpu
from jax.sharding import PartitionSpec as P

SWEEPS = 3
TOP_SWEEPS = 6
CYCLES = 2


OMEGA = 0.8
EXACT = lax.Precision.HIGHEST


def recv(value, steps, cyclic):
    count = lax.axis_size("gx")
    if cyclic:
        pairs = [(i, (i + steps) % count) for i in range(count)]
    else:
        pairs = [(i, i + steps) for i in range(count) if 0 <= i + steps < count]
    return lax.ppermute(value, "gx", pairs)


def inside(per_device, ghosts, length):
    count = lax.axis_size("gx")
    first = lax.axis_index("gx") * per_device - ghosts
    index = first + jnp.arange(length, dtype=jnp.int32)
    keep = (index >= 0) & (index < count * per_device)
    return keep.astype(jnp.float32)[:, None, None]


def exchange(to_right, to_left, steps, cyclic=False):
    arrays_r, arrays_l = list(to_right), list(to_left)
    shapes = [a.shape for a in arrays_r]
    stacked = all(shape[1:] == shapes[0][1:] for shape in shapes)
    if stacked:
        flat_r = jnp.concatenate(arrays_r)
        flat_l = jnp.concatenate(arrays_l)
    else:
        flat_r = jnp.concatenate([a.reshape(-1) for a in arrays_r])
        flat_l = jnp.concatenate([a.reshape(-1) for a in arrays_l])
    got_l, got_r = recv(flat_r, steps, cyclic), recv(flat_l, -steps, cyclic)

    def split(flat):
        out, at = [], 0
        for shape in shapes:
            if stacked:
                out.append(flat[at:at + shape[0]])
                at += shape[0]
            else:
                size = math.prod(shape)
                out.append(flat[at:at + size].reshape(shape))
                at += size
        return out

    return split(got_l), split(got_r)


def pair_matrix(extent):
    rows = jnp.arange(extent, dtype=jnp.int32)[:, None] // 2
    cols = jnp.arange(extent // 2, dtype=jnp.int32)[None, :]
    return (rows == cols).astype(jnp.float32)


def shrink_sides(field):
    extent_y = field.shape[1]
    extent_z = field.shape[2]
    along_z = jnp.einsum("xyz,zw->xyw", field, pair_matrix(extent_z), precision=EXACT)
    return jnp.einsum("xyw,yv->xvw", along_z, pair_matrix(extent_y), precision=EXACT)


def grow_sides(field):
    extent_y = field.shape[1]
    extent_z = field.shape[2]
    along_z = jnp.einsum("xyw,zw->xyz", field, pair_matrix(2 * extent_z), precision=EXACT)
    return jnp.einsum("xvz,yv->xyz", along_z, pair_matrix(2 * extent_y), precision=EXACT)


def coarsen(field):
    extent_x, extent_y, extent_z = field.shape
    planes = field.reshape(extent_x // 2, 2, extent_y, extent_z).sum(axis=1)
    return shrink_sides(planes) * 0.125


def refine(field):
    extent_x, extent_y, extent_z = field.shape
    wider = grow_sides(field)
    spread = jnp.broadcast_to(wider[:, None], (extent_x, 2, 2 * extent_y, 2 * extent_z))
    return spread.reshape(2 * extent_x, 2 * extent_y, 2 * extent_z)


def make_coefs(rho_ext, inv_spacing):
    two_s = 2.0 * inv_spacing
    center = rho_ext[1:-1]
    safe = jnp.where(center > 0, center, 1.0)
    padded = jnp.pad(center, ((0, 0), (1, 1), (1, 1)), mode="edge")
    near = [
        rho_ext[:-2],
        rho_ext[2:],
        padded[:, :-2, 1:-1],
        padded[:, 2:, 1:-1],
        padded[:, 1:-1, :-2],
        padded[:, 1:-1, 2:],
    ]
    faces = [two_s / (safe + jnp.where(nb > 0, nb, safe)) for nb in near]
    diag = faces[0] + faces[1] + faces[2] + faces[3] + faces[4] + faces[5]
    sides = faces[2:]
    lo, hi = rho_ext[:-1], rho_ext[1:]
    kxo = jnp.where((lo > 0) & (hi > 0), two_s / (lo + hi), 0.0)
    return {
        "kxo": kxo,
        "kyl": sides[0],
        "kyh": sides[1],
        "kzl": sides[2],
        "kzh": sides[3],
        "w": OMEGA / diag,
        "diag": diag,
    }


def side_terms(field, co, lo, hi):
    padded = jnp.pad(field, ((0, 0), (1, 1), (1, 1)))
    return (
        co["kyl"][lo:hi] * padded[:, :-2, 1:-1]
        + co["kyh"][lo:hi] * padded[:, 2:, 1:-1]
        + co["kzl"][lo:hi] * padded[:, 1:-1, :-2]
        + co["kzh"][lo:hi] * padded[:, 1:-1, 2:]
    )


def smooth(resid, co, sweeps):
    length = resid.shape[0]
    kxo = co["kxo"][1:-1]
    update = co["w"] * resid
    for sweep_no in range(1, sweeps):
        lo, hi = sweep_no, length - sweep_no
        inner = update[1:-1]
        off = (
            kxo[lo - 1:hi - 1] * update[:-2]
            + kxo[lo:hi] * update[2:]
            + side_terms(inner, co, lo, hi)
        )
        update = (1.0 - OMEGA) * inner + co["w"][lo:hi] * (resid[lo:hi] + off)
    return update


ROWS = 64
PAD = 8
VMEM_LIMIT = 64 * 1024 * 1024


def _zero_pads(buf):
    extent_y, extent_z = buf.shape[1] - 2 * PAD, buf.shape[2]
    zeros = jnp.zeros((PAD, extent_z), jnp.float32)

    def body(p, carry):
        buf[p, pl.ds(0, PAD), :] = zeros
        buf[p, pl.ds(PAD + extent_y, PAD), :] = zeros
        return carry

    lax.fori_loop(0, buf.shape[0], body, 0)


def _plane_loop(first, last, extent_y, body):
    def step(i, carry):
        for y0 in range(0, extent_y, ROWS):
            body(first + i, y0)
        return carry

    lax.fori_loop(0, last - first, step, 0)


def _neighbour_sum(src, at, y0, kxo_lo, kxo_hi, kyl, kyh, kzl, kzh):
    extent_z = src.shape[2]
    center = src[at, pl.ds(PAD + y0, ROWS), :]
    below = src[at, pl.ds(PAD + y0 - 1, ROWS), :]
    above = src[at, pl.ds(PAD + y0 + 1, ROWS), :]
    lanes = lax.broadcasted_iota(jnp.int32, center.shape, 1)
    left = jnp.where(lanes == 0, 0.0, pltpu.roll(center, 1, 1))
    right = jnp.where(lanes == extent_z - 1, 0.0, pltpu.roll(center, extent_z - 1, 1))
    off = (
        kxo_lo * src[at - 1, pl.ds(PAD + y0, ROWS), :]
        + kxo_hi * src[at + 1, pl.ds(PAD + y0, ROWS), :]
        + kyl * below
        + kyh * above
        + kzl * left
        + kzh * right
    )
    return center, off


def _smooth_in_vmem(resid, kxo, kyl, kyh, kzl, kzh, w, out, bufs, sweeps):
    length, extent_y = resid.shape[0], resid.shape[1]
    for buf in bufs:
        _zero_pads(buf)

    def first(q, y0):
        rows = pl.ds(y0, ROWS)
        bufs[0][q, pl.ds(PAD + y0, ROWS), :] = w[q, rows, :] * resid[q, rows, :]

    _plane_loop(0, length, extent_y, first)
    for sweep_no in range(1, sweeps):
        src = bufs[(sweep_no - 1) % 2]
        src_at = sweep_no - 1
        last = sweep_no == sweeps - 1
        dst = out if last else bufs[sweep_no % 2]
        dst_at = sweep_no

        def body(q, y0, src=src, src_at=src_at, dst=dst, dst_at=dst_at, last=last):
            rows = pl.ds(y0, ROWS)
            center, off = _neighbour_sum(
                src, q - src_at, y0, kxo[q - 1, rows, :], kxo[q, rows, :],
                kyl[q, rows, :], kyh[q, rows, :], kzl[q, rows, :], kzh[q, rows, :],
            )
            new = (1.0 - OMEGA) * center + w[q, rows, :] * (resid[q, rows, :] + off)
            if last:
                dst[q - dst_at, rows, :] = new
            else:
                dst[q - dst_at, pl.ds(PAD + y0, ROWS), :] = new

        _plane_loop(sweep_no, length - sweep_no, extent_y, body)


def _fine_first_kernel(resid, kxo, kyl, kyh, kzl, kzh, w, out, buf_a, buf_b):
    _smooth_in_vmem(resid, kxo, kyl, kyh, kzl, kzh, w, out, (buf_a, buf_b), SWEEPS)


def _fine_second_kernel(
    fine_ext, rhs, kxo_full, kyl, kyh, kzl, kzh, w, diag, out, resid_out, held, resid, buf_a, buf_b
):
    planes, extent_y = fine_ext.shape[0], fine_ext.shape[1]
    _zero_pads(held)

    def copy_in(q, y0):
        held[q, pl.ds(PAD + y0, ROWS), :] = fine_ext[q, pl.ds(y0, ROWS), :]

    _plane_loop(0, planes, extent_y, copy_in)

    def residual(q, y0):
        rows = pl.ds(y0, ROWS)
        center, off = _neighbour_sum(
            held, q + 1, y0, kxo_full[q, rows, :], kxo_full[q + 1, rows, :],
            kyl[q, rows, :], kyh[q, rows, :], kzl[q, rows, :], kzh[q, rows, :],
        )
        resid[q, rows, :] = rhs[q, rows, :] - (diag[q, rows, :] * center - off)

    _plane_loop(0, planes - 2, extent_y, residual)
    ghosts = SWEEPS - 1

    def copy_out(q, y0):
        rows = pl.ds(y0, ROWS)
        resid_out[q - ghosts, rows, :] = resid[q, rows, :]

    _plane_loop(ghosts, planes - 2 - ghosts, extent_y, copy_out)
    _smooth_in_vmem(
        resid, kxo_full.at[1:-1], kyl, kyh, kzl, kzh, w, out, (buf_a, buf_b), SWEEPS
    )


def _vmem_call(kernel, outs, scratch, *args):
    return pl.pallas_call(
        kernel,
        out_shape=outs,
        in_specs=[pl.BlockSpec(memory_space=pltpu.VMEM)] * len(args),
        out_specs=(
            [pl.BlockSpec(memory_space=pltpu.VMEM)] * len(outs)
            if isinstance(outs, (list, tuple))
            else pl.BlockSpec(memory_space=pltpu.VMEM)
        ),
        scratch_shapes=scratch,
        compiler_params=pltpu.CompilerParams(vmem_limit_bytes=VMEM_LIMIT),
    )(*args)


def fine_smooth(resid_ext, co):
    length, extent_y, extent_z = resid_ext.shape
    out = jax.ShapeDtypeStruct((length - 2 * (SWEEPS - 1), extent_y, extent_z), jnp.float32)
    padded = lambda planes: pltpu.VMEM((planes, extent_y + 2 * PAD, extent_z), jnp.float32)
    return _vmem_call(
        _fine_first_kernel, out, [padded(length), padded(length - 2)],
        resid_ext, co["kxo"][1:-1], co["kyl"], co["kyh"], co["kzl"], co["kzh"], co["w"],
    )


def fine_second(fine_ext, rhs_ext, co):
    planes, extent_y, extent_z = fine_ext.shape
    length = planes - 2
    block = length - 2 * (SWEEPS - 1)
    outs = [jax.ShapeDtypeStruct((block, extent_y, extent_z), jnp.float32)] * 2
    padded = lambda n: pltpu.VMEM((n, extent_y + 2 * PAD, extent_z), jnp.float32)
    return _vmem_call(
        _fine_second_kernel, outs,
        [padded(planes), pltpu.VMEM((length, extent_y, extent_z), jnp.float32),
         padded(length), padded(length - 2)],
        fine_ext, rhs_ext, co["kxo"], co["kyl"], co["kyh"], co["kzl"], co["kzh"], co["w"], co["diag"],
    )


def per_device(right_side, density):
    me = lax.axis_index("gx")

    (dl, rl), (dr, rr) = exchange(
        [density[-3:], right_side[-2:]], [density[:3], right_side[:2]], 1
    )
    rho0_ext = jnp.concatenate([dl, density, dr])
    rhs_ext = jnp.concatenate([rl, right_side, rr])
    co0 = make_coefs(rho0_ext, 1.0)

    fine_0 = fine_smooth(rhs_ext, co0)

    (fl,), (fr,) = exchange([fine_0[-3:]], [fine_0[:3]], 1)
    fine_ext = jnp.concatenate([fl, fine_0, fr])
    fine_1, resid_block = fine_second(fine_ext, rhs_ext, co0)

    rho1 = coarsen(density)
    rho2 = coarsen(rho1)
    rho3 = coarsen(rho2)

    def restrict(resid):
        r1 = coarsen(resid)
        r2 = coarsen(r1)
        return r1, r2, coarsen(r2)

    cycles = [restrict(right_side), restrict(resid_block)]
    to_right, to_left = [], []
    for r1, r2, _ in cycles:
        to_right += [r1[-2:], r2]
        to_left += [r1[:2], r2]
    to_right += [rho1[-3:], rho2]
    to_left += [rho1[:3], rho2]
    level3 = jnp.concatenate([r3 for _, _, r3 in cycles] + [rho3])
    to_right.append(level3)
    to_left.append(level3)
    got_l, got_r = exchange(to_right, to_left, 1, True)
    parts = []
    for k, (r1, r2, _) in enumerate(cycles):
        r1e = jnp.concatenate([got_l[2 * k], r1, got_r[2 * k]])
        r2e = jnp.concatenate([got_l[2 * k + 1], r2, got_r[2 * k + 1]])
        parts.append((r1e * inside(4, 2, r1e.shape[0]), r2e * inside(2, 2, r2e.shape[0])))
    at = 2 * len(cycles)
    rho1e = jnp.concatenate([got_l[at], rho1, got_r[at]])
    rho2_l, rho2_r = got_l[at + 1], got_r[at + 1]
    win3 = jnp.concatenate([got_l[-1], level3, got_r[-1]])
    got_l, got_r = exchange([win3, rho2_r[-1:]], [win3, rho2_l[:1]], 3, True)
    win9 = jnp.concatenate([got_l[0], win3, got_r[0]])
    rho2e = jnp.concatenate([got_l[1], rho2_l, rho2, rho2_r, got_r[1]])
    (got_l,), (got_r,) = exchange([win9], [win9], 9, True)
    win27 = jnp.concatenate([got_l, win9, got_r])
    per = len(cycles) + 1
    win27 = win27.reshape(27, per, win27.shape[1], win27.shape[2]) * inside(1, 13, 27)[:, None]
    windows = [win27[:, k] for k in range(per)]
    rho3w = windows[-1]

    co1 = make_coefs(rho1e * inside(4, 3, rho1e.shape[0]), 0.25)
    co2 = make_coefs(rho2e * inside(2, 3, rho2e.shape[0]), 0.25**2)
    center = 13
    co3 = make_coefs(rho3w[center - 3:center + 4], 0.25**3)
    pair_start = 1 - me % 2

    def to_top(window):
        return coarsen(lax.dynamic_slice_in_dim(window, pair_start, 2 * center))

    co4 = make_coefs(to_top(rho3w), 0.25**4)

    def coarse_part(r1e, r2e, r3w):
        top = smooth(to_top(r3w)[1:-1], co4, TOP_SWEEPS)
        summed = grow_sides(top) + smooth(r3w[center - 2:center + 3], co3, SWEEPS)
        summed = refine(summed) + smooth(r2e, co2, SWEEPS)
        summed = refine(summed) + smooth(r1e, co1, SWEEPS)
        return refine(summed)

    coarse_0 = coarse_part(parts[0][0], parts[0][1], windows[0])
    coarse_1 = coarse_part(parts[1][0], parts[1][1], windows[1])
    pressure = (fine_0 + fine_1) + coarse_0
    return (pressure, coarse_1)


def solution(mesh):
    return jax.shard_map(
        per_device,
        mesh=mesh,
        in_specs=(P("gx", None, None), P("gx", None, None)),
        out_specs=(P("gx", None, None), P("gx", None, None)),
        check_vma=False,
    )
```

```python
import math

import jax
import jax.numpy as jnp
from jax import lax
from jax.experimental import pallas as pl
from jax.experimental.pallas import tpu as pltpu
from jax.sharding import PartitionSpec as P

SWEEPS = 3
TOP_SWEEPS = 6
CYCLES = 2


OMEGA = 0.8
EXACT = lax.Precision.HIGHEST


def recv(value, steps, cyclic):
    count = lax.axis_size("gx")
    if cyclic:
        pairs = [(i, (i + steps) % count) for i in range(count)]
    else:
        pairs = [(i, i + steps) for i in range(count) if 0 <= i + steps < count]
    return lax.ppermute(value, "gx", pairs)


def inside(per_device, ghosts, length):
    count = lax.axis_size("gx")
    first = lax.axis_index("gx") * per_device - ghosts
    index = first + jnp.arange(length, dtype=jnp.int32)
    keep = (index >= 0) & (index < count * per_device)
    return keep.astype(jnp.float32)[:, None, None]


def exchange(to_right, to_left, steps, cyclic=False):
    arrays_r, arrays_l = list(to_right), list(to_left)
    shapes = [a.shape for a in arrays_r]
    stacked = all(shape[1:] == shapes[0][1:] for shape in shapes)
    if stacked:
        flat_r = jnp.concatenate(arrays_r)
        flat_l = jnp.concatenate(arrays_l)
    else:
        flat_r = jnp.concatenate([a.reshape(-1) for a in arrays_r])
        flat_l = jnp.concatenate([a.reshape(-1) for a in arrays_l])
    got_l, got_r = recv(flat_r, steps, cyclic), recv(flat_l, -steps, cyclic)

    def split(flat):
        out, at = [], 0
        for shape in shapes:
            if stacked:
                out.append(flat[at:at + shape[0]])
                at += shape[0]
            else:
                size = math.prod(shape)
                out.append(flat[at:at + size].reshape(shape))
                at += size
        return out

    return split(got_l), split(got_r)


def pair_matrix(extent):
    rows = jnp.arange(extent, dtype=jnp.int32)[:, None] // 2
    cols = jnp.arange(extent // 2, dtype=jnp.int32)[None, :]
    return (rows == cols).astype(jnp.float32)


def shrink_sides(field):
    extent_y = field.shape[1]
    extent_z = field.shape[2]
    along_z = jnp.einsum("xyz,zw->xyw", field, pair_matrix(extent_z), precision=EXACT)
    return jnp.einsum("xyw,yv->xvw", along_z, pair_matrix(extent_y), precision=EXACT)


def grow_sides(field):
    extent_y = field.shape[1]
    extent_z = field.shape[2]
    along_z = jnp.einsum("xyw,zw->xyz", field, pair_matrix(2 * extent_z), precision=EXACT)
    return jnp.einsum("xvz,yv->xyz", along_z, pair_matrix(2 * extent_y), precision=EXACT)


def coarsen(field):
    extent_x, extent_y, extent_z = field.shape
    planes = field.reshape(extent_x // 2, 2, extent_y, extent_z).sum(axis=1)
    return shrink_sides(planes) * 0.125


def refine(field):
    extent_x, extent_y, extent_z = field.shape
    wider = grow_sides(field)
    spread = jnp.broadcast_to(wider[:, None], (extent_x, 2, 2 * extent_y, 2 * extent_z))
    return spread.reshape(2 * extent_x, 2 * extent_y, 2 * extent_z)


def make_coefs(rho_ext, inv_spacing):
    two_s = 2.0 * inv_spacing
    center = rho_ext[1:-1]
    safe = jnp.where(center > 0, center, 1.0)
    padded = jnp.pad(center, ((0, 0), (1, 1), (1, 1)), mode="edge")
    near = [
        rho_ext[:-2],
        rho_ext[2:],
        padded[:, :-2, 1:-1],
        padded[:, 2:, 1:-1],
        padded[:, 1:-1, :-2],
        padded[:, 1:-1, 2:],
    ]
    faces = [two_s / (safe + jnp.where(nb > 0, nb, safe)) for nb in near]
    diag = faces[0] + faces[1] + faces[2] + faces[3] + faces[4] + faces[5]
    sides = faces[2:]
    lo, hi = rho_ext[:-1], rho_ext[1:]
    kxo = jnp.where((lo > 0) & (hi > 0), two_s / (lo + hi), 0.0)
    return {
        "kxo": kxo,
        "kyl": sides[0],
        "kyh": sides[1],
        "kzl": sides[2],
        "kzh": sides[3],
        "w": OMEGA / diag,
        "diag": diag,
    }


def side_terms(field, co, lo, hi):
    padded = jnp.pad(field, ((0, 0), (1, 1), (1, 1)))
    return (
        co["kyl"][lo:hi] * padded[:, :-2, 1:-1]
        + co["kyh"][lo:hi] * padded[:, 2:, 1:-1]
        + co["kzl"][lo:hi] * padded[:, 1:-1, :-2]
        + co["kzh"][lo:hi] * padded[:, 1:-1, 2:]
    )


def smooth(resid, co, sweeps):
    length = resid.shape[0]
    kxo = co["kxo"][1:-1]
    update = co["w"] * resid
    for sweep_no in range(1, sweeps):
        lo, hi = sweep_no, length - sweep_no
        inner = update[1:-1]
        off = (
            kxo[lo - 1:hi - 1] * update[:-2]
            + kxo[lo:hi] * update[2:]
            + side_terms(inner, co, lo, hi)
        )
        update = (1.0 - OMEGA) * inner + co["w"][lo:hi] * (resid[lo:hi] + off)
    return update


ROWS = 64
PAD = 8
VMEM_LIMIT = 64 * 1024 * 1024


def _zero_pads(buf):
    extent_y, extent_z = buf.shape[1] - 2 * PAD, buf.shape[2]
    zeros = jnp.zeros((PAD, extent_z), jnp.float32)

    def body(p, carry):
        buf[p, pl.ds(0, PAD), :] = zeros
        buf[p, pl.ds(PAD + extent_y, PAD), :] = zeros
        return carry

    lax.fori_loop(0, buf.shape[0], body, 0)


def _plane_loop(first, last, extent_y, body):
    def step(i, carry):
        for y0 in range(0, extent_y, ROWS):
            body(first + i, y0)
        return carry

    lax.fori_loop(0, last - first, step, 0)


def _neighbour_sum(src, at, y0, kxo_lo, kxo_hi, kyl, kyh, kzl, kzh):
    extent_z = src.shape[2]
    center = src[at, pl.ds(PAD + y0, ROWS), :]
    below = src[at, pl.ds(PAD + y0 - 1, ROWS), :]
    above = src[at, pl.ds(PAD + y0 + 1, ROWS), :]
    lanes = lax.broadcasted_iota(jnp.int32, center.shape, 1)
    left = jnp.where(lanes == 0, 0.0, pltpu.roll(center, 1, 1))
    right = jnp.where(lanes == extent_z - 1, 0.0, pltpu.roll(center, extent_z - 1, 1))
    off = (
        kxo_lo * src[at - 1, pl.ds(PAD + y0, ROWS), :]
        + kxo_hi * src[at + 1, pl.ds(PAD + y0, ROWS), :]
        + kyl * below
        + kyh * above
        + kzl * left
        + kzh * right
    )
    return center, off


def _smooth_in_vmem(resid, kxo, kyl, kyh, kzl, kzh, w, out, bufs, sweeps):
    length, extent_y = resid.shape[0], resid.shape[1]
    for buf in bufs:
        _zero_pads(buf)

    def first(q, y0):
        rows = pl.ds(y0, ROWS)
        bufs[0][q, pl.ds(PAD + y0, ROWS), :] = w[q, rows, :] * resid[q, rows, :]

    _plane_loop(0, length, extent_y, first)
    for sweep_no in range(1, sweeps):
        src = bufs[(sweep_no - 1) % 2]
        src_at = sweep_no - 1
        last = sweep_no == sweeps - 1
        dst = out if last else bufs[sweep_no % 2]
        dst_at = sweep_no

        def body(q, y0, src=src, src_at=src_at, dst=dst, dst_at=dst_at, last=last):
            rows = pl.ds(y0, ROWS)
            center, off = _neighbour_sum(
                src, q - src_at, y0, kxo[q - 1, rows, :], kxo[q, rows, :],
                kyl[q, rows, :], kyh[q, rows, :], kzl[q, rows, :], kzh[q, rows, :],
            )
            new = (1.0 - OMEGA) * center + w[q, rows, :] * (resid[q, rows, :] + off)
            if last:
                dst[q - dst_at, rows, :] = new
            else:
                dst[q - dst_at, pl.ds(PAD + y0, ROWS), :] = new

        _plane_loop(sweep_no, length - sweep_no, extent_y, body)


def _fine_first_kernel(resid, kxo_full, kyl, kyh, kzl, kzh, w, out, low, high, buf_a, buf_b):
    _smooth_in_vmem(resid, kxo_full.at[1:-1], kyl, kyh, kzl, kzh, w, out, (buf_a, buf_b), SWEEPS)
    width, block, extent_y = low.shape[0], out.shape[0], out.shape[1]

    def edges(q, y0):
        rows = pl.ds(y0, ROWS)
        low[q, rows, :] = out[q, rows, :]
        high[q, rows, :] = out[block - width + q, rows, :]

    _plane_loop(0, width, extent_y, edges)


def _fine_second_kernel(
    fine_l, fine, fine_r, rhs, kxo_full, kyl, kyh, kzl, kzh, w, diag, out, resid_out, held, resid,
    buf_a, buf_b,
):
    width, block, extent_y = fine_l.shape[0], fine.shape[0], fine.shape[1]
    planes = held.shape[0]
    _zero_pads(held)
    for src, first in ((fine_l, 0), (fine, width), (fine_r, width + block)):

        def copy_in(q, y0, src=src, first=first):
            held[q, pl.ds(PAD + y0, ROWS), :] = src[q - first, pl.ds(y0, ROWS), :]

        _plane_loop(first, first + src.shape[0], extent_y, copy_in)

    def residual(q, y0):
        rows = pl.ds(y0, ROWS)
        center, off = _neighbour_sum(
            held, q + 1, y0, kxo_full[q, rows, :], kxo_full[q + 1, rows, :],
            kyl[q, rows, :], kyh[q, rows, :], kzl[q, rows, :], kzh[q, rows, :],
        )
        resid[q, rows, :] = rhs[q, rows, :] - (diag[q, rows, :] * center - off)

    _plane_loop(0, planes - 2, extent_y, residual)
    ghosts = SWEEPS - 1

    def copy_out(q, y0):
        rows = pl.ds(y0, ROWS)
        resid_out[q - ghosts, rows, :] = resid[q, rows, :]

    _plane_loop(ghosts, planes - 2 - ghosts, extent_y, copy_out)
    _smooth_in_vmem(
        resid, kxo_full.at[1:-1], kyl, kyh, kzl, kzh, w, out, (buf_a, buf_b), SWEEPS
    )


def _vmem_call(kernel, outs, scratch, *args):
    return pl.pallas_call(
        kernel,
        out_shape=outs,
        in_specs=[pl.BlockSpec(memory_space=pltpu.VMEM)] * len(args),
        out_specs=(
            [pl.BlockSpec(memory_space=pltpu.VMEM)] * len(outs)
            if isinstance(outs, (list, tuple))
            else pl.BlockSpec(memory_space=pltpu.VMEM)
        ),
        scratch_shapes=scratch,
        compiler_params=pltpu.CompilerParams(vmem_limit_bytes=VMEM_LIMIT),
    )(*args)


def fine_smooth(resid_ext, co, width):
    length, extent_y, extent_z = resid_ext.shape
    outs = [
        jax.ShapeDtypeStruct((length - 2 * (SWEEPS - 1), extent_y, extent_z), jnp.float32),
        jax.ShapeDtypeStruct((width, extent_y, extent_z), jnp.float32),
        jax.ShapeDtypeStruct((width, extent_y, extent_z), jnp.float32),
    ]
    padded = lambda planes: pltpu.VMEM((planes, extent_y + 2 * PAD, extent_z), jnp.float32)
    return _vmem_call(
        _fine_first_kernel, outs, [padded(length), padded(length - 2)],
        resid_ext, co["kxo"], co["kyl"], co["kyh"], co["kzl"], co["kzh"], co["w"],
    )


def fine_second(fine_l, fine, fine_r, rhs_ext, co):
    extent_y, extent_z = fine.shape[1], fine.shape[2]
    planes = fine.shape[0] + 2 * fine_l.shape[0]
    length = planes - 2
    block = length - 2 * (SWEEPS - 1)
    outs = [jax.ShapeDtypeStruct((block, extent_y, extent_z), jnp.float32)] * 2
    padded = lambda n: pltpu.VMEM((n, extent_y + 2 * PAD, extent_z), jnp.float32)
    return _vmem_call(
        _fine_second_kernel, outs,
        [padded(planes), pltpu.VMEM((length, extent_y, extent_z), jnp.float32),
         padded(length), padded(length - 2)],
        fine_l, fine, fine_r, rhs_ext, co["kxo"], co["kyl"], co["kyh"], co["kzl"], co["kzh"], co["w"], co["diag"],
    )


def per_device(right_side, density):
    me = lax.axis_index("gx")

    (dl, rl), (dr, rr) = exchange(
        [density[-3:], right_side[-2:]], [density[:3], right_side[:2]], 1
    )
    rho0_ext = jnp.concatenate([dl, density, dr])
    rhs_ext = jnp.concatenate([rl, right_side, rr])
    co0 = make_coefs(rho0_ext, 1.0)

    fine_0, low, high = fine_smooth(rhs_ext, co0, 3)

    (fl,), (fr,) = exchange([high], [low], 1)
    fine_1, resid_block = fine_second(fl, fine_0, fr, rhs_ext, co0)

    rho1 = coarsen(density)
    rho2 = coarsen(rho1)
    rho3 = coarsen(rho2)

    def restrict(resid):
        r1 = coarsen(resid)
        r2 = coarsen(r1)
        return r1, r2, coarsen(r2)

    cycles = [restrict(right_side), restrict(resid_block)]
    to_right, to_left = [], []
    for r1, r2, _ in cycles:
        to_right += [r1[-2:], r2]
        to_left += [r1[:2], r2]
    to_right += [rho1[-3:], rho2]
    to_left += [rho1[:3], rho2]
    level3 = jnp.concatenate([r3 for _, _, r3 in cycles] + [rho3])
    to_right.append(level3)
    to_left.append(level3)
    got_l, got_r = exchange(to_right, to_left, 1, True)
    parts = []
    for k, (r1, r2, _) in enumerate(cycles):
        r1e = jnp.concatenate([got_l[2 * k], r1, got_r[2 * k]])
        r2e = jnp.concatenate([got_l[2 * k + 1], r2, got_r[2 * k + 1]])
        parts.append((r1e * inside(4, 2, r1e.shape[0]), r2e * inside(2, 2, r2e.shape[0])))
    at = 2 * len(cycles)
    rho1e = jnp.concatenate([got_l[at], rho1, got_r[at]])
    rho2_l, rho2_r = got_l[at + 1], got_r[at + 1]
    win3 = jnp.concatenate([got_l[-1], level3, got_r[-1]])
    got_l, got_r = exchange([win3, rho2_r[-1:]], [win3, rho2_l[:1]], 3, True)
    win9 = jnp.concatenate([got_l[0], win3, got_r[0]])
    rho2e = jnp.concatenate([got_l[1], rho2_l, rho2, rho2_r, got_r[1]])
    (got_l,), (got_r,) = exchange([win9], [win9], 9, True)
    win27 = jnp.concatenate([got_l, win9, got_r])
    per = len(cycles) + 1
    win27 = win27.reshape(27, per, win27.shape[1], win27.shape[2]) * inside(1, 13, 27)[:, None]
    windows = [win27[:, k] for k in range(per)]
    rho3w = windows[-1]

    co1 = make_coefs(rho1e * inside(4, 3, rho1e.shape[0]), 0.25)
    co2 = make_coefs(rho2e * inside(2, 3, rho2e.shape[0]), 0.25**2)
    center = 13
    co3 = make_coefs(rho3w[center - 3:center + 4], 0.25**3)
    pair_start = 1 - me % 2

    def to_top(window):
        return coarsen(lax.dynamic_slice_in_dim(window, pair_start, 2 * center))

    co4 = make_coefs(to_top(rho3w), 0.25**4)

    def coarse_part(r1e, r2e, r3w):
        top = smooth(to_top(r3w)[1:-1], co4, TOP_SWEEPS)
        summed = grow_sides(top) + smooth(r3w[center - 2:center + 3], co3, SWEEPS)
        summed = refine(summed) + smooth(r2e, co2, SWEEPS)
        summed = refine(summed) + smooth(r1e, co1, SWEEPS)
        return refine(summed)

    coarse_0 = coarse_part(parts[0][0], parts[0][1], windows[0])
    coarse_1 = coarse_part(parts[1][0], parts[1][1], windows[1])
    pressure = (fine_0 + fine_1) + coarse_0
    return (pressure, coarse_1)


def solution(mesh):
    return jax.shard_map(
        per_device,
        mesh=mesh,
        in_specs=(P("gx", None, None), P("gx", None, None)),
        out_specs=(P("gx", None, None), P("gx", None, None)),
        check_vma=False,
    )
```

```python
import math

import jax
import jax.numpy as jnp
from jax import lax
from jax.experimental import pallas as pl
from jax.experimental.pallas import tpu as pltpu
from jax.sharding import PartitionSpec as P

SWEEPS = 3
TOP_SWEEPS = 6
CYCLES = 2


OMEGA = 0.8
EXACT = lax.Precision.HIGHEST


def recv(value, steps, cyclic):
    count = lax.axis_size("gx")
    if cyclic:
        pairs = [(i, (i + steps) % count) for i in range(count)]
    else:
        pairs = [(i, i + steps) for i in range(count) if 0 <= i + steps < count]
    return lax.ppermute(value, "gx", pairs)


def inside(per_device, ghosts, length):
    count = lax.axis_size("gx")
    first = lax.axis_index("gx") * per_device - ghosts
    index = first + jnp.arange(length, dtype=jnp.int32)
    keep = (index >= 0) & (index < count * per_device)
    return keep.astype(jnp.float32)[:, None, None]


def exchange(to_right, to_left, steps, cyclic=False):
    arrays_r, arrays_l = list(to_right), list(to_left)
    shapes = [a.shape for a in arrays_r]
    stacked = all(shape[1:] == shapes[0][1:] for shape in shapes)
    if stacked:
        flat_r = jnp.concatenate(arrays_r)
        flat_l = jnp.concatenate(arrays_l)
    else:
        flat_r = jnp.concatenate([a.reshape(-1) for a in arrays_r])
        flat_l = jnp.concatenate([a.reshape(-1) for a in arrays_l])
    got_l, got_r = recv(flat_r, steps, cyclic), recv(flat_l, -steps, cyclic)

    def split(flat):
        out, at = [], 0
        for shape in shapes:
            if stacked:
                out.append(flat[at:at + shape[0]])
                at += shape[0]
            else:
                size = math.prod(shape)
                out.append(flat[at:at + size].reshape(shape))
                at += size
        return out

    return split(got_l), split(got_r)


def pair_matrix(extent):
    rows = jnp.arange(extent, dtype=jnp.int32)[:, None] // 2
    cols = jnp.arange(extent // 2, dtype=jnp.int32)[None, :]
    return (rows == cols).astype(jnp.float32)


def shrink_sides(field):
    extent_y = field.shape[1]
    extent_z = field.shape[2]
    along_z = jnp.einsum("xyz,zw->xyw", field, pair_matrix(extent_z), precision=EXACT)
    return jnp.einsum("xyw,yv->xvw", along_z, pair_matrix(extent_y), precision=EXACT)


def grow_sides(field):
    extent_y = field.shape[1]
    extent_z = field.shape[2]
    along_z = jnp.einsum("xyw,zw->xyz", field, pair_matrix(2 * extent_z), precision=EXACT)
    return jnp.einsum("xvz,yv->xyz", along_z, pair_matrix(2 * extent_y), precision=EXACT)


def coarsen(field):
    extent_x, extent_y, extent_z = field.shape
    planes = field.reshape(extent_x // 2, 2, extent_y, extent_z).sum(axis=1)
    return shrink_sides(planes) * 0.125


def refine(field):
    extent_x, extent_y, extent_z = field.shape
    wider = grow_sides(field)
    spread = jnp.broadcast_to(wider[:, None], (extent_x, 2, 2 * extent_y, 2 * extent_z))
    return spread.reshape(2 * extent_x, 2 * extent_y, 2 * extent_z)


def make_coefs(rho_ext, inv_spacing):
    two_s = 2.0 * inv_spacing
    center = rho_ext[1:-1]
    safe = jnp.where(center > 0, center, 1.0)
    padded = jnp.pad(center, ((0, 0), (1, 1), (1, 1)), mode="edge")
    near = [
        rho_ext[:-2],
        rho_ext[2:],
        padded[:, :-2, 1:-1],
        padded[:, 2:, 1:-1],
        padded[:, 1:-1, :-2],
        padded[:, 1:-1, 2:],
    ]
    faces = [two_s / (safe + jnp.where(nb > 0, nb, safe)) for nb in near]
    diag = faces[0] + faces[1] + faces[2] + faces[3] + faces[4] + faces[5]
    sides = faces[2:]
    lo, hi = rho_ext[:-1], rho_ext[1:]
    kxo = jnp.where((lo > 0) & (hi > 0), two_s / (lo + hi), 0.0)
    return {
        "kxo": kxo,
        "kyl": sides[0],
        "kyh": sides[1],
        "kzl": sides[2],
        "kzh": sides[3],
        "w": OMEGA / diag,
        "diag": diag,
    }


def side_terms(field, co, lo, hi):
    padded = jnp.pad(field, ((0, 0), (1, 1), (1, 1)))
    return (
        co["kyl"][lo:hi] * padded[:, :-2, 1:-1]
        + co["kyh"][lo:hi] * padded[:, 2:, 1:-1]
        + co["kzl"][lo:hi] * padded[:, 1:-1, :-2]
        + co["kzh"][lo:hi] * padded[:, 1:-1, 2:]
    )


def smooth(resid, co, sweeps):
    length = resid.shape[0]
    kxo = co["kxo"][1:-1]
    update = co["w"] * resid
    for sweep_no in range(1, sweeps):
        lo, hi = sweep_no, length - sweep_no
        inner = update[1:-1]
        off = (
            kxo[lo - 1:hi - 1] * update[:-2]
            + kxo[lo:hi] * update[2:]
            + side_terms(inner, co, lo, hi)
        )
        update = (1.0 - OMEGA) * inner + co["w"][lo:hi] * (resid[lo:hi] + off)
    return update


ROWS = 64
PAD = 8
VMEM_LIMIT = 64 * 1024 * 1024


def _zero_pads(buf):
    extent_y, extent_z = buf.shape[1] - 2 * PAD, buf.shape[2]
    zeros = jnp.zeros((PAD, extent_z), jnp.float32)

    def body(p, carry):
        buf[p, pl.ds(0, PAD), :] = zeros
        buf[p, pl.ds(PAD + extent_y, PAD), :] = zeros
        return carry

    lax.fori_loop(0, buf.shape[0], body, 0)


def _plane_loop(first, last, extent_y, body):
    def step(i, carry):
        for y0 in range(0, extent_y, ROWS):
            body(first + i, y0)
        return carry

    lax.fori_loop(0, last - first, step, 0)


def _neighbour_sum(src, at, y0, kxo_lo, kxo_hi, kyl, kyh, kzl, kzh):
    extent_z = src.shape[2]
    center = src[at, pl.ds(PAD + y0, ROWS), :]
    below = src[at, pl.ds(PAD + y0 - 1, ROWS), :]
    above = src[at, pl.ds(PAD + y0 + 1, ROWS), :]
    lanes = lax.broadcasted_iota(jnp.int32, center.shape, 1)
    left = jnp.where(lanes == 0, 0.0, pltpu.roll(center, 1, 1))
    right = jnp.where(lanes == extent_z - 1, 0.0, pltpu.roll(center, extent_z - 1, 1))
    off = (
        kxo_lo * src[at - 1, pl.ds(PAD + y0, ROWS), :]
        + kxo_hi * src[at + 1, pl.ds(PAD + y0, ROWS), :]
        + kyl * below
        + kyh * above
        + kzl * left
        + kzh * right
    )
    return center, off


def _smooth_in_vmem(resid, kxo, kyl, kyh, kzl, kzh, w, out, bufs, sweeps):
    length, extent_y = resid.shape[0], resid.shape[1]
    for buf in bufs:
        _zero_pads(buf)

    def first(q, y0):
        rows = pl.ds(y0, ROWS)
        bufs[0][q, pl.ds(PAD + y0, ROWS), :] = w[q, rows, :] * resid[q, rows, :]

    _plane_loop(0, length, extent_y, first)
    for sweep_no in range(1, sweeps):
        src = bufs[(sweep_no - 1) % 2]
        src_at = sweep_no - 1
        last = sweep_no == sweeps - 1
        dst = out if last else bufs[sweep_no % 2]
        dst_at = sweep_no

        def body(q, y0, src=src, src_at=src_at, dst=dst, dst_at=dst_at, last=last):
            rows = pl.ds(y0, ROWS)
            center, off = _neighbour_sum(
                src, q - src_at, y0, kxo[q - 1, rows, :], kxo[q, rows, :],
                kyl[q, rows, :], kyh[q, rows, :], kzl[q, rows, :], kzh[q, rows, :],
            )
            new = (1.0 - OMEGA) * center + w[q, rows, :] * (resid[q, rows, :] + off)
            if last:
                dst[q - dst_at, rows, :] = new
            else:
                dst[q - dst_at, pl.ds(PAD + y0, ROWS), :] = new

        _plane_loop(sweep_no, length - sweep_no, extent_y, body)


def _fine_first_kernel(resid, kxo_full, kyl, kyh, kzl, kzh, w, out, low, high, buf_a, buf_b):
    _smooth_in_vmem(resid, kxo_full.at[1:-1], kyl, kyh, kzl, kzh, w, out, (buf_a, buf_b), SWEEPS)
    width, block, extent_y = low.shape[0], out.shape[0], out.shape[1]

    def edges(q, y0):
        rows = pl.ds(y0, ROWS)
        low[q, rows, :] = out[q, rows, :]
        high[q, rows, :] = out[block - width + q, rows, :]

    _plane_loop(0, width, extent_y, edges)


def _fine_second_kernel(
    fine_l, fine, fine_r, rhs, kxo_full, kyl, kyh, kzl, kzh, w, diag, out, resid_out, held, resid,
    buf_a, buf_b,
):
    width, block, extent_y = fine_l.shape[0], fine.shape[0], fine.shape[1]
    planes = held.shape[0]
    _zero_pads(held)
    for src, first in ((fine_l, 0), (fine, width), (fine_r, width + block)):

        def copy_in(q, y0, src=src, first=first):
            held[q, pl.ds(PAD + y0, ROWS), :] = src[q - first, pl.ds(y0, ROWS), :]

        _plane_loop(first, first + src.shape[0], extent_y, copy_in)

    def residual(q, y0):
        rows = pl.ds(y0, ROWS)
        center, off = _neighbour_sum(
            held, q + 1, y0, kxo_full[q, rows, :], kxo_full[q + 1, rows, :],
            kyl[q, rows, :], kyh[q, rows, :], kzl[q, rows, :], kzh[q, rows, :],
        )
        resid[q, rows, :] = rhs[q, rows, :] - (diag[q, rows, :] * center - off)

    _plane_loop(0, planes - 2, extent_y, residual)
    ghosts = SWEEPS - 1

    def copy_out(q, y0):
        rows = pl.ds(y0, ROWS)
        resid_out[q - ghosts, rows, :] = resid[q, rows, :]

    _plane_loop(ghosts, planes - 2 - ghosts, extent_y, copy_out)
    _smooth_in_vmem(
        resid, kxo_full.at[1:-1], kyl, kyh, kzl, kzh, w, out, (buf_a, buf_b), SWEEPS
    )


def _vmem_call(kernel, outs, scratch, *args):
    return pl.pallas_call(
        kernel,
        out_shape=outs,
        in_specs=[pl.BlockSpec(memory_space=pltpu.VMEM)] * len(args),
        out_specs=(
            [pl.BlockSpec(memory_space=pltpu.VMEM)] * len(outs)
            if isinstance(outs, (list, tuple))
            else pl.BlockSpec(memory_space=pltpu.VMEM)
        ),
        scratch_shapes=scratch,
        compiler_params=pltpu.CompilerParams(vmem_limit_bytes=VMEM_LIMIT),
    )(*args)


def fine_smooth(resid_ext, co, width):
    length, extent_y, extent_z = resid_ext.shape
    outs = [
        jax.ShapeDtypeStruct((length - 2 * (SWEEPS - 1), extent_y, extent_z), jnp.float32),
        jax.ShapeDtypeStruct((width, extent_y, extent_z), jnp.float32),
        jax.ShapeDtypeStruct((width, extent_y, extent_z), jnp.float32),
    ]
    padded = lambda planes: pltpu.VMEM((planes, extent_y + 2 * PAD, extent_z), jnp.float32)
    return _vmem_call(
        _fine_first_kernel, outs, [padded(length), padded(length - 2)],
        resid_ext, co["kxo"], co["kyl"], co["kyh"], co["kzl"], co["kzh"], co["w"],
    )


def fine_second(fine_l, fine, fine_r, rhs_ext, co):
    extent_y, extent_z = fine.shape[1], fine.shape[2]
    planes = fine.shape[0] + 2 * fine_l.shape[0]
    length = planes - 2
    block = length - 2 * (SWEEPS - 1)
    outs = [jax.ShapeDtypeStruct((block, extent_y, extent_z), jnp.float32)] * 2
    padded = lambda n: pltpu.VMEM((n, extent_y + 2 * PAD, extent_z), jnp.float32)
    return _vmem_call(
        _fine_second_kernel, outs,
        [padded(planes), pltpu.VMEM((length, extent_y, extent_z), jnp.float32),
         padded(length), padded(length - 2)],
        fine_l, fine, fine_r, rhs_ext, co["kxo"], co["kyl"], co["kyh"], co["kzl"], co["kzh"], co["w"], co["diag"],
    )


def per_device(right_side, density):
    me = lax.axis_index("gx")

    dl, dr = recv(density[-3:], 1, False), recv(density[:3], -1, False)
    rl, rr = recv(right_side[-2:], 1, False), recv(right_side[:2], -1, False)
    rho0_ext = jnp.concatenate([dl, density, dr])
    rhs_ext = jnp.concatenate([rl, right_side, rr])
    co0 = make_coefs(rho0_ext, 1.0)

    fine_0, low, high = fine_smooth(rhs_ext, co0, 3)

    (fl,), (fr,) = exchange([high], [low], 1)
    fine_1, resid_block = fine_second(fl, fine_0, fr, rhs_ext, co0)

    rho1 = coarsen(density)
    rho2 = coarsen(rho1)
    rho3 = coarsen(rho2)

    def restrict(resid):
        r1 = coarsen(resid)
        r2 = coarsen(r1)
        return r1, r2, coarsen(r2)

    cycles = [restrict(right_side), restrict(resid_block)]
    to_right, to_left = [], []
    for r1, r2, _ in cycles:
        to_right += [r1[-2:], r2]
        to_left += [r1[:2], r2]
    to_right += [rho1[-3:], rho2]
    to_left += [rho1[:3], rho2]
    level3 = jnp.concatenate([r3 for _, _, r3 in cycles] + [rho3])
    to_right.append(level3)
    to_left.append(level3)
    got_l, got_r = exchange(to_right, to_left, 1, True)
    parts = []
    for k, (r1, r2, _) in enumerate(cycles):
        r1e = jnp.concatenate([got_l[2 * k], r1, got_r[2 * k]])
        r2e = jnp.concatenate([got_l[2 * k + 1], r2, got_r[2 * k + 1]])
        parts.append((r1e * inside(4, 2, r1e.shape[0]), r2e * inside(2, 2, r2e.shape[0])))
    at = 2 * len(cycles)
    rho1e = jnp.concatenate([got_l[at], rho1, got_r[at]])
    rho2_l, rho2_r = got_l[at + 1], got_r[at + 1]
    win3 = jnp.concatenate([got_l[-1], level3, got_r[-1]])
    got_l, got_r = exchange([win3, rho2_r[-1:]], [win3, rho2_l[:1]], 3, True)
    win9 = jnp.concatenate([got_l[0], win3, got_r[0]])
    rho2e = jnp.concatenate([got_l[1], rho2_l, rho2, rho2_r, got_r[1]])
    (got_l,), (got_r,) = exchange([win9], [win9], 9, True)
    win27 = jnp.concatenate([got_l, win9, got_r])
    per = len(cycles) + 1
    win27 = win27.reshape(27, per, win27.shape[1], win27.shape[2]) * inside(1, 13, 27)[:, None]
    windows = [win27[:, k] for k in range(per)]
    rho3w = windows[-1]

    co1 = make_coefs(rho1e * inside(4, 3, rho1e.shape[0]), 0.25)
    co2 = make_coefs(rho2e * inside(2, 3, rho2e.shape[0]), 0.25**2)
    center = 13
    co3 = make_coefs(rho3w[center - 3:center + 4], 0.25**3)
    pair_start = 1 - me % 2

    def to_top(window):
        return coarsen(lax.dynamic_slice_in_dim(window, pair_start, 2 * center))

    co4 = make_coefs(to_top(rho3w), 0.25**4)

    def coarse_part(r1e, r2e, r3w):
        top = smooth(to_top(r3w)[1:-1], co4, TOP_SWEEPS)
        summed = grow_sides(top) + smooth(r3w[center - 2:center + 3], co3, SWEEPS)
        summed = refine(summed) + smooth(r2e, co2, SWEEPS)
        summed = refine(summed) + smooth(r1e, co1, SWEEPS)
        return refine(summed)

    coarse_0 = coarse_part(parts[0][0], parts[0][1], windows[0])
    coarse_1 = coarse_part(parts[1][0], parts[1][1], windows[1])
    pressure = (fine_0 + fine_1) + coarse_0
    return (pressure, coarse_1)


def solution(mesh):
    return jax.shard_map(
        per_device,
        mesh=mesh,
        in_specs=(P("gx", None, None), P("gx", None, None)),
        out_specs=(P("gx", None, None), P("gx", None, None)),
        check_vma=False,
    )
```

```python
import math

import jax
import jax.numpy as jnp
from jax import lax
from jax.experimental import pallas as pl
from jax.experimental.pallas import tpu as pltpu
from jax.sharding import PartitionSpec as P

SWEEPS = 3
TOP_SWEEPS = 6
CYCLES = 2


OMEGA = 0.8
EXACT = lax.Precision.HIGHEST


def recv(value, steps, cyclic):
    count = lax.axis_size("gx")
    if cyclic:
        pairs = [(i, (i + steps) % count) for i in range(count)]
    else:
        pairs = [(i, i + steps) for i in range(count) if 0 <= i + steps < count]
    return lax.ppermute(value, "gx", pairs)


def inside(per_device, ghosts, length):
    count = lax.axis_size("gx")
    first = lax.axis_index("gx") * per_device - ghosts
    index = first + jnp.arange(length, dtype=jnp.int32)
    keep = (index >= 0) & (index < count * per_device)
    return keep.astype(jnp.float32)[:, None, None]


def exchange(to_right, to_left, steps, cyclic=False):
    arrays_r, arrays_l = list(to_right), list(to_left)
    shapes = [a.shape for a in arrays_r]
    stacked = all(shape[1:] == shapes[0][1:] for shape in shapes)
    if stacked:
        flat_r = jnp.concatenate(arrays_r)
        flat_l = jnp.concatenate(arrays_l)
    else:
        flat_r = jnp.concatenate([a.reshape(-1) for a in arrays_r])
        flat_l = jnp.concatenate([a.reshape(-1) for a in arrays_l])
    got_l, got_r = recv(flat_r, steps, cyclic), recv(flat_l, -steps, cyclic)

    def split(flat):
        out, at = [], 0
        for shape in shapes:
            if stacked:
                out.append(flat[at:at + shape[0]])
                at += shape[0]
            else:
                size = math.prod(shape)
                out.append(flat[at:at + size].reshape(shape))
                at += size
        return out

    return split(got_l), split(got_r)


def pair_matrix(extent):
    rows = jnp.arange(extent, dtype=jnp.int32)[:, None] // 2
    cols = jnp.arange(extent // 2, dtype=jnp.int32)[None, :]
    return (rows == cols).astype(jnp.float32)


def shrink_sides(field):
    extent_y = field.shape[1]
    extent_z = field.shape[2]
    along_z = jnp.einsum("xyz,zw->xyw", field, pair_matrix(extent_z), precision=EXACT)
    return jnp.einsum("xyw,yv->xvw", along_z, pair_matrix(extent_y), precision=EXACT)


def grow_sides(field):
    extent_y = field.shape[1]
    extent_z = field.shape[2]
    along_z = jnp.einsum("xyw,zw->xyz", field, pair_matrix(2 * extent_z), precision=EXACT)
    return jnp.einsum("xvz,yv->xyz", along_z, pair_matrix(2 * extent_y), precision=EXACT)


def coarsen(field):
    extent_x, extent_y, extent_z = field.shape
    planes = field.reshape(extent_x // 2, 2, extent_y, extent_z).sum(axis=1)
    return shrink_sides(planes) * 0.125


def refine(field):
    extent_x, extent_y, extent_z = field.shape
    wider = grow_sides(field)
    spread = jnp.broadcast_to(wider[:, None], (extent_x, 2, 2 * extent_y, 2 * extent_z))
    return spread.reshape(2 * extent_x, 2 * extent_y, 2 * extent_z)


def make_coefs(rho_ext, inv_spacing):
    two_s = 2.0 * inv_spacing
    center = rho_ext[1:-1]
    safe = jnp.where(center > 0, center, 1.0)
    padded = jnp.pad(center, ((0, 0), (1, 1), (1, 1)), mode="edge")
    near = [
        rho_ext[:-2],
        rho_ext[2:],
        padded[:, :-2, 1:-1],
        padded[:, 2:, 1:-1],
        padded[:, 1:-1, :-2],
        padded[:, 1:-1, 2:],
    ]
    faces = [two_s / (safe + jnp.where(nb > 0, nb, safe)) for nb in near]
    diag = faces[0] + faces[1] + faces[2] + faces[3] + faces[4] + faces[5]
    sides = faces[2:]
    lo, hi = rho_ext[:-1], rho_ext[1:]
    kxo = jnp.where((lo > 0) & (hi > 0), two_s / (lo + hi), 0.0)
    return {
        "kxo": kxo,
        "kyl": sides[0],
        "kyh": sides[1],
        "kzl": sides[2],
        "kzh": sides[3],
        "w": OMEGA / diag,
        "diag": diag,
    }


def side_terms(field, co, lo, hi):
    padded = jnp.pad(field, ((0, 0), (1, 1), (1, 1)))
    return (
        co["kyl"][lo:hi] * padded[:, :-2, 1:-1]
        + co["kyh"][lo:hi] * padded[:, 2:, 1:-1]
        + co["kzl"][lo:hi] * padded[:, 1:-1, :-2]
        + co["kzh"][lo:hi] * padded[:, 1:-1, 2:]
    )


def smooth(resid, co, sweeps):
    length = resid.shape[0]
    kxo = co["kxo"][1:-1]
    update = co["w"] * resid
    for sweep_no in range(1, sweeps):
        lo, hi = sweep_no, length - sweep_no
        inner = update[1:-1]
        off = (
            kxo[lo - 1:hi - 1] * update[:-2]
            + kxo[lo:hi] * update[2:]
            + side_terms(inner, co, lo, hi)
        )
        update = (1.0 - OMEGA) * inner + co["w"][lo:hi] * (resid[lo:hi] + off)
    return update


ROWS = 128
PAD = 8
VMEM_LIMIT = 64 * 1024 * 1024


def _zero_pads(buf):
    extent_y, extent_z = buf.shape[1] - 2 * PAD, buf.shape[2]
    zeros = jnp.zeros((PAD, extent_z), jnp.float32)

    def body(p, carry):
        buf[p, pl.ds(0, PAD), :] = zeros
        buf[p, pl.ds(PAD + extent_y, PAD), :] = zeros
        return carry

    lax.fori_loop(0, buf.shape[0], body, 0)


def _plane_loop(first, last, extent_y, body):
    def step(i, carry):
        for y0 in range(0, extent_y, ROWS):
            body(first + i, y0)
        return carry

    lax.fori_loop(0, last - first, step, 0)


def _neighbour_sum(src, at, y0, kxo_lo, kxo_hi, kyl, kyh, kzl, kzh):
    extent_z = src.shape[2]
    center = src[at, pl.ds(PAD + y0, ROWS), :]
    below = src[at, pl.ds(PAD + y0 - 1, ROWS), :]
    above = src[at, pl.ds(PAD + y0 + 1, ROWS), :]
    lanes = lax.broadcasted_iota(jnp.int32, center.shape, 1)
    left = jnp.where(lanes == 0, 0.0, pltpu.roll(center, 1, 1))
    right = jnp.where(lanes == extent_z - 1, 0.0, pltpu.roll(center, extent_z - 1, 1))
    off = (
        kxo_lo * src[at - 1, pl.ds(PAD + y0, ROWS), :]
        + kxo_hi * src[at + 1, pl.ds(PAD + y0, ROWS), :]
        + kyl * below
        + kyh * above
        + kzl * left
        + kzh * right
    )
    return center, off


def _smooth_in_vmem(resid, kxo, kyl, kyh, kzl, kzh, w, out, bufs, sweeps):
    length, extent_y = resid.shape[0], resid.shape[1]
    for buf in bufs:
        _zero_pads(buf)

    def first(q, y0):
        rows = pl.ds(y0, ROWS)
        bufs[0][q, pl.ds(PAD + y0, ROWS), :] = w[q, rows, :] * resid[q, rows, :]

    _plane_loop(0, length, extent_y, first)
    for sweep_no in range(1, sweeps):
        src = bufs[(sweep_no - 1) % 2]
        src_at = sweep_no - 1
        last = sweep_no == sweeps - 1
        dst = out if last else bufs[sweep_no % 2]
        dst_at = sweep_no

        def body(q, y0, src=src, src_at=src_at, dst=dst, dst_at=dst_at, last=last):
            rows = pl.ds(y0, ROWS)
            center, off = _neighbour_sum(
                src, q - src_at, y0, kxo[q - 1, rows, :], kxo[q, rows, :],
                kyl[q, rows, :], kyh[q, rows, :], kzl[q, rows, :], kzh[q, rows, :],
            )
            new = (1.0 - OMEGA) * center + w[q, rows, :] * (resid[q, rows, :] + off)
            if last:
                dst[q - dst_at, rows, :] = new
            else:
                dst[q - dst_at, pl.ds(PAD + y0, ROWS), :] = new

        _plane_loop(sweep_no, length - sweep_no, extent_y, body)


def _fine_first_kernel(resid, kxo_full, kyl, kyh, kzl, kzh, w, out, low, high, buf_a, buf_b):
    _smooth_in_vmem(resid, kxo_full.at[1:-1], kyl, kyh, kzl, kzh, w, out, (buf_a, buf_b), SWEEPS)
    width, block, extent_y = low.shape[0], out.shape[0], out.shape[1]

    def edges(q, y0):
        rows = pl.ds(y0, ROWS)
        low[q, rows, :] = out[q, rows, :]
        high[q, rows, :] = out[block - width + q, rows, :]

    _plane_loop(0, width, extent_y, edges)


def _fine_second_kernel(
    fine_l, fine, fine_r, rhs, kxo_full, kyl, kyh, kzl, kzh, w, diag, out, resid_out, held, resid,
    buf_a, buf_b,
):
    width, block, extent_y = fine_l.shape[0], fine.shape[0], fine.shape[1]
    planes = held.shape[0]
    _zero_pads(held)
    for src, first in ((fine_l, 0), (fine, width), (fine_r, width + block)):

        def copy_in(q, y0, src=src, first=first):
            held[q, pl.ds(PAD + y0, ROWS), :] = src[q - first, pl.ds(y0, ROWS), :]

        _plane_loop(first, first + src.shape[0], extent_y, copy_in)

    def residual(q, y0):
        rows = pl.ds(y0, ROWS)
        center, off = _neighbour_sum(
            held, q + 1, y0, kxo_full[q, rows, :], kxo_full[q + 1, rows, :],
            kyl[q, rows, :], kyh[q, rows, :], kzl[q, rows, :], kzh[q, rows, :],
        )
        resid[q, rows, :] = rhs[q, rows, :] - (diag[q, rows, :] * center - off)

    _plane_loop(0, planes - 2, extent_y, residual)
    ghosts = SWEEPS - 1

    def copy_out(q, y0):
        rows = pl.ds(y0, ROWS)
        resid_out[q - ghosts, rows, :] = resid[q, rows, :]

    _plane_loop(ghosts, planes - 2 - ghosts, extent_y, copy_out)
    _smooth_in_vmem(
        resid, kxo_full.at[1:-1], kyl, kyh, kzl, kzh, w, out, (buf_a, buf_b), SWEEPS
    )


def _vmem_call(kernel, outs, scratch, *args):
    return pl.pallas_call(
        kernel,
        out_shape=outs,
        in_specs=[pl.BlockSpec(memory_space=pltpu.VMEM)] * len(args),
        out_specs=(
            [pl.BlockSpec(memory_space=pltpu.VMEM)] * len(outs)
            if isinstance(outs, (list, tuple))
            else pl.BlockSpec(memory_space=pltpu.VMEM)
        ),
        scratch_shapes=scratch,
        compiler_params=pltpu.CompilerParams(vmem_limit_bytes=VMEM_LIMIT),
    )(*args)


def fine_smooth(resid_ext, co, width):
    length, extent_y, extent_z = resid_ext.shape
    outs = [
        jax.ShapeDtypeStruct((length - 2 * (SWEEPS - 1), extent_y, extent_z), jnp.float32),
        jax.ShapeDtypeStruct((width, extent_y, extent_z), jnp.float32),
        jax.ShapeDtypeStruct((width, extent_y, extent_z), jnp.float32),
    ]
    padded = lambda planes: pltpu.VMEM((planes, extent_y + 2 * PAD, extent_z), jnp.float32)
    return _vmem_call(
        _fine_first_kernel, outs, [padded(length), padded(length - 2)],
        resid_ext, co["kxo"], co["kyl"], co["kyh"], co["kzl"], co["kzh"], co["w"],
    )


def fine_second(fine_l, fine, fine_r, rhs_ext, co):
    extent_y, extent_z = fine.shape[1], fine.shape[2]
    planes = fine.shape[0] + 2 * fine_l.shape[0]
    length = planes - 2
    block = length - 2 * (SWEEPS - 1)
    outs = [jax.ShapeDtypeStruct((block, extent_y, extent_z), jnp.float32)] * 2
    padded = lambda n: pltpu.VMEM((n, extent_y + 2 * PAD, extent_z), jnp.float32)
    return _vmem_call(
        _fine_second_kernel, outs,
        [padded(planes), pltpu.VMEM((length, extent_y, extent_z), jnp.float32),
         padded(length), padded(length - 2)],
        fine_l, fine, fine_r, rhs_ext, co["kxo"], co["kyl"], co["kyh"], co["kzl"], co["kzh"], co["w"], co["diag"],
    )


def per_device(right_side, density):
    me = lax.axis_index("gx")

    (dl, rl), (dr, rr) = exchange(
        [density[-3:], right_side[-2:]], [density[:3], right_side[:2]], 1
    )
    rho0_ext = jnp.concatenate([dl, density, dr])
    rhs_ext = jnp.concatenate([rl, right_side, rr])
    co0 = make_coefs(rho0_ext, 1.0)

    fine_0, low, high = fine_smooth(rhs_ext, co0, 3)

    (fl,), (fr,) = exchange([high], [low], 1)
    fine_1, resid_block = fine_second(fl, fine_0, fr, rhs_ext, co0)

    rho1 = coarsen(density)
    rho2 = coarsen(rho1)
    rho3 = coarsen(rho2)

    def restrict(resid):
        r1 = coarsen(resid)
        r2 = coarsen(r1)
        return r1, r2, coarsen(r2)

    cycles = [restrict(right_side), restrict(resid_block)]
    to_right, to_left = [], []
    for r1, r2, _ in cycles:
        to_right += [r1[-2:], r2]
        to_left += [r1[:2], r2]
    to_right += [rho1[-3:], rho2]
    to_left += [rho1[:3], rho2]
    level3 = jnp.concatenate([r3 for _, _, r3 in cycles] + [rho3])
    to_right.append(level3)
    to_left.append(level3)
    got_l, got_r = exchange(to_right, to_left, 1, True)
    parts = []
    for k, (r1, r2, _) in enumerate(cycles):
        r1e = jnp.concatenate([got_l[2 * k], r1, got_r[2 * k]])
        r2e = jnp.concatenate([got_l[2 * k + 1], r2, got_r[2 * k + 1]])
        parts.append((r1e * inside(4, 2, r1e.shape[0]), r2e * inside(2, 2, r2e.shape[0])))
    at = 2 * len(cycles)
    rho1e = jnp.concatenate([got_l[at], rho1, got_r[at]])
    rho2_l, rho2_r = got_l[at + 1], got_r[at + 1]
    win3 = jnp.concatenate([got_l[-1], level3, got_r[-1]])
    got_l, got_r = exchange([win3, rho2_r[-1:]], [win3, rho2_l[:1]], 3, True)
    win9 = jnp.concatenate([got_l[0], win3, got_r[0]])
    rho2e = jnp.concatenate([got_l[1], rho2_l, rho2, rho2_r, got_r[1]])
    (got_l,), (got_r,) = exchange([win9], [win9], 9, True)
    win27 = jnp.concatenate([got_l, win9, got_r])
    per = len(cycles) + 1
    win27 = win27.reshape(27, per, win27.shape[1], win27.shape[2]) * inside(1, 13, 27)[:, None]
    windows = [win27[:, k] for k in range(per)]
    rho3w = windows[-1]

    co1 = make_coefs(rho1e * inside(4, 3, rho1e.shape[0]), 0.25)
    co2 = make_coefs(rho2e * inside(2, 3, rho2e.shape[0]), 0.25**2)
    center = 13
    co3 = make_coefs(rho3w[center - 3:center + 4], 0.25**3)
    pair_start = 1 - me % 2

    def to_top(window):
        return coarsen(lax.dynamic_slice_in_dim(window, pair_start, 2 * center))

    co4 = make_coefs(to_top(rho3w), 0.25**4)

    def coarse_part(r1e, r2e, r3w):
        top = smooth(to_top(r3w)[1:-1], co4, TOP_SWEEPS)
        summed = grow_sides(top) + smooth(r3w[center - 2:center + 3], co3, SWEEPS)
        summed = refine(summed) + smooth(r2e, co2, SWEEPS)
        summed = refine(summed) + smooth(r1e, co1, SWEEPS)
        return refine(summed)

    coarse_0 = coarse_part(parts[0][0], parts[0][1], windows[0])
    coarse_1 = coarse_part(parts[1][0], parts[1][1], windows[1])
    pressure = (fine_0 + fine_1) + coarse_0
    return (pressure, coarse_1)


def solution(mesh):
    return jax.shard_map(
        per_device,
        mesh=mesh,
        in_specs=(P("gx", None, None), P("gx", None, None)),
        out_specs=(P("gx", None, None), P("gx", None, None)),
        check_vma=False,
    )
```

```python
import math

import jax
import jax.numpy as jnp
from jax import lax
from jax.experimental import pallas as pl
from jax.experimental.pallas import tpu as pltpu
from jax.sharding import PartitionSpec as P

SWEEPS = 3
TOP_SWEEPS = 6
CYCLES = 2


OMEGA = 0.8
EXACT = lax.Precision.HIGHEST


def recv(value, steps, cyclic):
    count = lax.axis_size("gx")
    if cyclic:
        pairs = [(i, (i + steps) % count) for i in range(count)]
    else:
        pairs = [(i, i + steps) for i in range(count) if 0 <= i + steps < count]
    return lax.ppermute(value, "gx", pairs)


def inside(per_device, ghosts, length):
    count = lax.axis_size("gx")
    first = lax.axis_index("gx") * per_device - ghosts
    index = first + jnp.arange(length, dtype=jnp.int32)
    keep = (index >= 0) & (index < count * per_device)
    return keep.astype(jnp.float32)[:, None, None]


def exchange(to_right, to_left, steps, cyclic=False):
    arrays_r, arrays_l = list(to_right), list(to_left)
    shapes = [a.shape for a in arrays_r]
    stacked = all(shape[1:] == shapes[0][1:] for shape in shapes)
    if stacked:
        flat_r = jnp.concatenate(arrays_r)
        flat_l = jnp.concatenate(arrays_l)
    else:
        flat_r = jnp.concatenate([a.reshape(-1) for a in arrays_r])
        flat_l = jnp.concatenate([a.reshape(-1) for a in arrays_l])
    got_l, got_r = recv(flat_r, steps, cyclic), recv(flat_l, -steps, cyclic)

    def split(flat):
        out, at = [], 0
        for shape in shapes:
            if stacked:
                out.append(flat[at:at + shape[0]])
                at += shape[0]
            else:
                size = math.prod(shape)
                out.append(flat[at:at + size].reshape(shape))
                at += size
        return out

    return split(got_l), split(got_r)


def pair_matrix(extent):
    rows = jnp.arange(extent, dtype=jnp.int32)[:, None] // 2
    cols = jnp.arange(extent // 2, dtype=jnp.int32)[None, :]
    return (rows == cols).astype(jnp.float32)


def shrink_sides(field):
    extent_y = field.shape[1]
    extent_z = field.shape[2]
    along_z = jnp.einsum("xyz,zw->xyw", field, pair_matrix(extent_z), precision=EXACT)
    return jnp.einsum("xyw,yv->xvw", along_z, pair_matrix(extent_y), precision=EXACT)


def grow_sides(field):
    extent_y = field.shape[1]
    extent_z = field.shape[2]
    along_z = jnp.einsum("xyw,zw->xyz", field, pair_matrix(2 * extent_z), precision=EXACT)
    return jnp.einsum("xvz,yv->xyz", along_z, pair_matrix(2 * extent_y), precision=EXACT)


def coarsen(field):
    extent_x, extent_y, extent_z = field.shape
    planes = field.reshape(extent_x // 2, 2, extent_y, extent_z).sum(axis=1)
    return shrink_sides(planes) * 0.125


def refine(field):
    extent_x, extent_y, extent_z = field.shape
    wider = grow_sides(field)
    spread = jnp.broadcast_to(wider[:, None], (extent_x, 2, 2 * extent_y, 2 * extent_z))
    return spread.reshape(2 * extent_x, 2 * extent_y, 2 * extent_z)


def make_coefs(rho_ext, inv_spacing):
    two_s = 2.0 * inv_spacing
    center = rho_ext[1:-1]
    safe = jnp.where(center > 0, center, 1.0)
    padded = jnp.pad(center, ((0, 0), (1, 1), (1, 1)), mode="edge")
    near = [
        rho_ext[:-2],
        rho_ext[2:],
        padded[:, :-2, 1:-1],
        padded[:, 2:, 1:-1],
        padded[:, 1:-1, :-2],
        padded[:, 1:-1, 2:],
    ]
    faces = [two_s / (safe + jnp.where(nb > 0, nb, safe)) for nb in near]
    diag = faces[0] + faces[1] + faces[2] + faces[3] + faces[4] + faces[5]
    sides = faces[2:]
    lo, hi = rho_ext[:-1], rho_ext[1:]
    kxo = jnp.where((lo > 0) & (hi > 0), two_s / (lo + hi), 0.0)
    return {
        "kxo": kxo,
        "kyl": sides[0],
        "kyh": sides[1],
        "kzl": sides[2],
        "kzh": sides[3],
        "w": OMEGA / diag,
        "diag": diag,
    }


def side_terms(field, co, lo, hi):
    padded = jnp.pad(field, ((0, 0), (1, 1), (1, 1)))
    return (
        co["kyl"][lo:hi] * padded[:, :-2, 1:-1]
        + co["kyh"][lo:hi] * padded[:, 2:, 1:-1]
        + co["kzl"][lo:hi] * padded[:, 1:-1, :-2]
        + co["kzh"][lo:hi] * padded[:, 1:-1, 2:]
    )


def smooth(resid, co, sweeps):
    length = resid.shape[0]
    kxo = co["kxo"][1:-1]
    update = co["w"] * resid
    for sweep_no in range(1, sweeps):
        lo, hi = sweep_no, length - sweep_no
        inner = update[1:-1]
        off = (
            kxo[lo - 1:hi - 1] * update[:-2]
            + kxo[lo:hi] * update[2:]
            + side_terms(inner, co, lo, hi)
        )
        update = (1.0 - OMEGA) * inner + co["w"][lo:hi] * (resid[lo:hi] + off)
    return update


ROWS = 64
PAD = 8
VMEM_LIMIT = 64 * 1024 * 1024


def _zero_pads(buf):
    extent_y, extent_z = buf.shape[1] - 2 * PAD, buf.shape[2]
    zeros = jnp.zeros((PAD, extent_z), jnp.float32)

    def body(p, carry):
        buf[p, pl.ds(0, PAD), :] = zeros
        buf[p, pl.ds(PAD + extent_y, PAD), :] = zeros
        return carry

    lax.fori_loop(0, buf.shape[0], body, 0)


def _plane_loop(first, last, extent_y, body):
    def step(i, carry):
        for y0 in range(0, extent_y, ROWS):
            body(first + i, y0)
        return carry

    lax.fori_loop(0, last - first, step, 0)


def _neighbour_sum(src, at, y0, kxo_lo, kxo_hi, kyl, kyh, kzl, kzh):
    extent_z = src.shape[2]
    center = src[at, pl.ds(PAD + y0, ROWS), :]
    below = src[at, pl.ds(PAD + y0 - 1, ROWS), :]
    above = src[at, pl.ds(PAD + y0 + 1, ROWS), :]
    lanes = lax.broadcasted_iota(jnp.int32, center.shape, 1)
    left = jnp.where(lanes == 0, 0.0, pltpu.roll(center, 1, 1))
    right = jnp.where(lanes == extent_z - 1, 0.0, pltpu.roll(center, extent_z - 1, 1))
    off = (
        kxo_lo * src[at - 1, pl.ds(PAD + y0, ROWS), :]
        + kxo_hi * src[at + 1, pl.ds(PAD + y0, ROWS), :]
        + kyl * below
        + kyh * above
        + kzl * left
        + kzh * right
    )
    return center, off


def _smooth_in_vmem(resid, kxo, kyl, kyh, kzl, kzh, w, out, bufs, sweeps):
    length, extent_y = resid.shape[0], resid.shape[1]
    for buf in bufs:
        _zero_pads(buf)

    def first(q, y0):
        rows = pl.ds(y0, ROWS)
        bufs[0][q, pl.ds(PAD + y0, ROWS), :] = w[q, rows, :] * resid[q, rows, :]

    _plane_loop(0, length, extent_y, first)
    for sweep_no in range(1, sweeps):
        src = bufs[(sweep_no - 1) % 2]
        src_at = sweep_no - 1
        last = sweep_no == sweeps - 1
        dst = out if last else bufs[sweep_no % 2]
        dst_at = sweep_no

        def body(q, y0, src=src, src_at=src_at, dst=dst, dst_at=dst_at, last=last):
            rows = pl.ds(y0, ROWS)
            center, off = _neighbour_sum(
                src, q - src_at, y0, kxo[q - 1, rows, :], kxo[q, rows, :],
                kyl[q, rows, :], kyh[q, rows, :], kzl[q, rows, :], kzh[q, rows, :],
            )
            new = (1.0 - OMEGA) * center + w[q, rows, :] * (resid[q, rows, :] + off)
            if last:
                dst[q - dst_at, rows, :] = new
            else:
                dst[q - dst_at, pl.ds(PAD + y0, ROWS), :] = new

        _plane_loop(sweep_no, length - sweep_no, extent_y, body)


def _fine_first_kernel(resid, kxo_full, kyl, kyh, kzl, kzh, w, out, low, high, buf_a, buf_b):
    _smooth_in_vmem(resid, kxo_full.at[1:-1], kyl, kyh, kzl, kzh, w, out, (buf_a, buf_b), SWEEPS)
    width, block, extent_y = low.shape[0], out.shape[0], out.shape[1]

    def edges(q, y0):
        rows = pl.ds(y0, ROWS)
        low[q, rows, :] = out[q, rows, :]
        high[q, rows, :] = out[block - width + q, rows, :]

    _plane_loop(0, width, extent_y, edges)


def _fine_second_kernel(
    fine_l, fine, fine_r, rhs, kxo_full, kyl, kyh, kzl, kzh, w, diag, out, resid_out, held, resid,
    buf_a, buf_b,
):
    width, block, extent_y = fine_l.shape[0], fine.shape[0], fine.shape[1]
    planes = held.shape[0]
    _zero_pads(held)
    for src, first in ((fine_l, 0), (fine, width), (fine_r, width + block)):

        def copy_in(q, y0, src=src, first=first):
            held[q, pl.ds(PAD + y0, ROWS), :] = src[q - first, pl.ds(y0, ROWS), :]

        _plane_loop(first, first + src.shape[0], extent_y, copy_in)

    ghosts = SWEEPS - 1

    def residual(q, y0, keep=False):
        rows = pl.ds(y0, ROWS)
        center, off = _neighbour_sum(
            held, q + 1, y0, kxo_full[q, rows, :], kxo_full[q + 1, rows, :],
            kyl[q, rows, :], kyh[q, rows, :], kzl[q, rows, :], kzh[q, rows, :],
        )
        value = rhs[q, rows, :] - (diag[q, rows, :] * center - off)
        resid[q, rows, :] = value
        if keep:
            resid_out[q - ghosts, rows, :] = value

    _plane_loop(0, ghosts, extent_y, residual)
    _plane_loop(ghosts, planes - 2 - ghosts, extent_y, lambda q, y0: residual(q, y0, True))
    _plane_loop(planes - 2 - ghosts, planes - 2, extent_y, residual)
    _smooth_in_vmem(
        resid, kxo_full.at[1:-1], kyl, kyh, kzl, kzh, w, out, (buf_a, buf_b), SWEEPS
    )


def _vmem_call(kernel, outs, scratch, *args):
    return pl.pallas_call(
        kernel,
        out_shape=outs,
        in_specs=[pl.BlockSpec(memory_space=pltpu.VMEM)] * len(args),
        out_specs=(
            [pl.BlockSpec(memory_space=pltpu.VMEM)] * len(outs)
            if isinstance(outs, (list, tuple))
            else pl.BlockSpec(memory_space=pltpu.VMEM)
        ),
        scratch_shapes=scratch,
        compiler_params=pltpu.CompilerParams(vmem_limit_bytes=VMEM_LIMIT),
    )(*args)


def fine_smooth(resid_ext, co, width):
    length, extent_y, extent_z = resid_ext.shape
    outs = [
        jax.ShapeDtypeStruct((length - 2 * (SWEEPS - 1), extent_y, extent_z), jnp.float32),
        jax.ShapeDtypeStruct((width, extent_y, extent_z), jnp.float32),
        jax.ShapeDtypeStruct((width, extent_y, extent_z), jnp.float32),
    ]
    padded = lambda planes: pltpu.VMEM((planes, extent_y + 2 * PAD, extent_z), jnp.float32)
    return _vmem_call(
        _fine_first_kernel, outs, [padded(length), padded(length - 2)],
        resid_ext, co["kxo"], co["kyl"], co["kyh"], co["kzl"], co["kzh"], co["w"],
    )


def fine_second(fine_l, fine, fine_r, rhs_ext, co):
    extent_y, extent_z = fine.shape[1], fine.shape[2]
    planes = fine.shape[0] + 2 * fine_l.shape[0]
    length = planes - 2
    block = length - 2 * (SWEEPS - 1)
    outs = [jax.ShapeDtypeStruct((block, extent_y, extent_z), jnp.float32)] * 2
    padded = lambda n: pltpu.VMEM((n, extent_y + 2 * PAD, extent_z), jnp.float32)
    return _vmem_call(
        _fine_second_kernel, outs,
        [padded(planes), pltpu.VMEM((length, extent_y, extent_z), jnp.float32),
         padded(length), padded(length - 2)],
        fine_l, fine, fine_r, rhs_ext, co["kxo"], co["kyl"], co["kyh"], co["kzl"], co["kzh"], co["w"], co["diag"],
    )


def per_device(right_side, density):
    me = lax.axis_index("gx")

    (dl, rl), (dr, rr) = exchange(
        [density[-3:], right_side[-2:]], [density[:3], right_side[:2]], 1
    )
    rho0_ext = jnp.concatenate([dl, density, dr])
    rhs_ext = jnp.concatenate([rl, right_side, rr])
    co0 = make_coefs(rho0_ext, 1.0)

    fine_0, low, high = fine_smooth(rhs_ext, co0, 3)

    (fl,), (fr,) = exchange([high], [low], 1)
    fine_1, resid_block = fine_second(fl, fine_0, fr, rhs_ext, co0)

    rho1 = coarsen(density)
    rho2 = coarsen(rho1)
    rho3 = coarsen(rho2)

    def restrict(resid):
        r1 = coarsen(resid)
        r2 = coarsen(r1)
        return r1, r2, coarsen(r2)

    cycles = [restrict(right_side), restrict(resid_block)]
    to_right, to_left = [], []
    for r1, r2, _ in cycles:
        to_right += [r1[-2:], r2]
        to_left += [r1[:2], r2]
    to_right += [rho1[-3:], rho2]
    to_left += [rho1[:3], rho2]
    level3 = jnp.concatenate([r3 for _, _, r3 in cycles] + [rho3])
    to_right.append(level3)
    to_left.append(level3)
    got_l, got_r = exchange(to_right, to_left, 1, True)
    parts = []
    for k, (r1, r2, _) in enumerate(cycles):
        r1e = jnp.concatenate([got_l[2 * k], r1, got_r[2 * k]])
        r2e = jnp.concatenate([got_l[2 * k + 1], r2, got_r[2 * k + 1]])
        parts.append((r1e * inside(4, 2, r1e.shape[0]), r2e * inside(2, 2, r2e.shape[0])))
    at = 2 * len(cycles)
    rho1e = jnp.concatenate([got_l[at], rho1, got_r[at]])
    rho2_l, rho2_r = got_l[at + 1], got_r[at + 1]
    win3 = jnp.concatenate([got_l[-1], level3, got_r[-1]])
    got_l, got_r = exchange([win3, rho2_r[-1:]], [win3, rho2_l[:1]], 3, True)
    win9 = jnp.concatenate([got_l[0], win3, got_r[0]])
    rho2e = jnp.concatenate([got_l[1], rho2_l, rho2, rho2_r, got_r[1]])
    (got_l,), (got_r,) = exchange([win9], [win9], 9, True)
    win27 = jnp.concatenate([got_l, win9, got_r])
    per = len(cycles) + 1
    win27 = win27.reshape(27, per, win27.shape[1], win27.shape[2]) * inside(1, 13, 27)[:, None]
    windows = [win27[:, k] for k in range(per)]
    rho3w = windows[-1]

    co1 = make_coefs(rho1e * inside(4, 3, rho1e.shape[0]), 0.25)
    co2 = make_coefs(rho2e * inside(2, 3, rho2e.shape[0]), 0.25**2)
    center = 13
    co3 = make_coefs(rho3w[center - 3:center + 4], 0.25**3)
    pair_start = 1 - me % 2

    def to_top(window):
        return coarsen(lax.dynamic_slice_in_dim(window, pair_start, 2 * center))

    co4 = make_coefs(to_top(rho3w), 0.25**4)

    def coarse_part(r1e, r2e, r3w):
        top = smooth(to_top(r3w)[1:-1], co4, TOP_SWEEPS)
        summed = grow_sides(top) + smooth(r3w[center - 2:center + 3], co3, SWEEPS)
        summed = refine(summed) + smooth(r2e, co2, SWEEPS)
        summed = refine(summed) + smooth(r1e, co1, SWEEPS)
        return refine(summed)

    coarse_0 = coarse_part(parts[0][0], parts[0][1], windows[0])
    coarse_1 = coarse_part(parts[1][0], parts[1][1], windows[1])
    pressure = (fine_0 + fine_1) + coarse_0
    return (pressure, coarse_1)


def solution(mesh):
    return jax.shard_map(
        per_device,
        mesh=mesh,
        in_specs=(P("gx", None, None), P("gx", None, None)),
        out_specs=(P("gx", None, None), P("gx", None, None)),
        check_vma=False,
    )
```

```python
import math

import jax
import jax.numpy as jnp
from jax import lax
from jax.experimental import pallas as pl
from jax.experimental.pallas import tpu as pltpu
from jax.sharding import PartitionSpec as P

SWEEPS = 3
TOP_SWEEPS = 6
CYCLES = 2


OMEGA = 0.8
EXACT = lax.Precision.HIGHEST


def recv(value, steps, cyclic):
    count = lax.axis_size("gx")
    if cyclic:
        pairs = [(i, (i + steps) % count) for i in range(count)]
    else:
        pairs = [(i, i + steps) for i in range(count) if 0 <= i + steps < count]
    return lax.ppermute(value, "gx", pairs)


def inside(per_device, ghosts, length):
    count = lax.axis_size("gx")
    first = lax.axis_index("gx") * per_device - ghosts
    index = first + jnp.arange(length, dtype=jnp.int32)
    keep = (index >= 0) & (index < count * per_device)
    return keep.astype(jnp.float32)[:, None, None]


def exchange(to_right, to_left, steps, cyclic=False):
    arrays_r, arrays_l = list(to_right), list(to_left)
    shapes = [a.shape for a in arrays_r]
    stacked = all(shape[1:] == shapes[0][1:] for shape in shapes)
    if stacked:
        flat_r = jnp.concatenate(arrays_r)
        flat_l = jnp.concatenate(arrays_l)
    else:
        flat_r = jnp.concatenate([a.reshape(-1) for a in arrays_r])
        flat_l = jnp.concatenate([a.reshape(-1) for a in arrays_l])
    got_l, got_r = recv(flat_r, steps, cyclic), recv(flat_l, -steps, cyclic)

    def split(flat):
        out, at = [], 0
        for shape in shapes:
            if stacked:
                out.append(flat[at:at + shape[0]])
                at += shape[0]
            else:
                size = math.prod(shape)
                out.append(flat[at:at + size].reshape(shape))
                at += size
        return out

    return split(got_l), split(got_r)


def pair_matrix(extent):
    rows = jnp.arange(extent, dtype=jnp.int32)[:, None] // 2
    cols = jnp.arange(extent // 2, dtype=jnp.int32)[None, :]
    return (rows == cols).astype(jnp.float32)


def shrink_sides(field):
    extent_y = field.shape[1]
    extent_z = field.shape[2]
    along_z = jnp.einsum("xyz,zw->xyw", field, pair_matrix(extent_z), precision=EXACT)
    return jnp.einsum("xyw,yv->xvw", along_z, pair_matrix(extent_y), precision=EXACT)


def grow_sides(field):
    extent_y = field.shape[1]
    extent_z = field.shape[2]
    along_z = jnp.einsum("xyw,zw->xyz", field, pair_matrix(2 * extent_z), precision=EXACT)
    return jnp.einsum("xvz,yv->xyz", along_z, pair_matrix(2 * extent_y), precision=EXACT)


def coarsen(field):
    extent_x, extent_y, extent_z = field.shape
    planes = field.reshape(extent_x // 2, 2, extent_y, extent_z).sum(axis=1)
    return shrink_sides(planes) * 0.125


def refine(field):
    extent_x, extent_y, extent_z = field.shape
    wider = grow_sides(field)
    spread = jnp.broadcast_to(wider[:, None], (extent_x, 2, 2 * extent_y, 2 * extent_z))
    return spread.reshape(2 * extent_x, 2 * extent_y, 2 * extent_z)


def make_coefs(rho_ext, inv_spacing):
    two_s = 2.0 * inv_spacing
    center = rho_ext[1:-1]
    safe = jnp.where(center > 0, center, 1.0)
    padded = jnp.pad(center, ((0, 0), (1, 1), (1, 1)), mode="edge")
    near = [
        rho_ext[:-2],
        rho_ext[2:],
        padded[:, :-2, 1:-1],
        padded[:, 2:, 1:-1],
        padded[:, 1:-1, :-2],
        padded[:, 1:-1, 2:],
    ]
    faces = [two_s / (safe + jnp.where(nb > 0, nb, safe)) for nb in near]
    diag = faces[0] + faces[1] + faces[2] + faces[3] + faces[4] + faces[5]
    sides = faces[2:]
    lo, hi = rho_ext[:-1], rho_ext[1:]
    kxo = jnp.where((lo > 0) & (hi > 0), two_s / (lo + hi), 0.0)
    return {
        "kxo": kxo,
        "kyl": sides[0],
        "kyh": sides[1],
        "kzl": sides[2],
        "kzh": sides[3],
        "w": OMEGA / diag,
        "diag": diag,
    }


def side_terms(field, co, lo, hi):
    padded = jnp.pad(field, ((0, 0), (1, 1), (1, 1)))
    return (
        co["kyl"][lo:hi] * padded[:, :-2, 1:-1]
        + co["kyh"][lo:hi] * padded[:, 2:, 1:-1]
        + co["kzl"][lo:hi] * padded[:, 1:-1, :-2]
        + co["kzh"][lo:hi] * padded[:, 1:-1, 2:]
    )


def smooth(resid, co, sweeps):
    length = resid.shape[0]
    kxo = co["kxo"][1:-1]
    update = co["w"] * resid
    for sweep_no in range(1, sweeps):
        lo, hi = sweep_no, length - sweep_no
        inner = update[1:-1]
        off = (
            kxo[lo - 1:hi - 1] * update[:-2]
            + kxo[lo:hi] * update[2:]
            + side_terms(inner, co, lo, hi)
        )
        update = (1.0 - OMEGA) * inner + co["w"][lo:hi] * (resid[lo:hi] + off)
    return update


ROWS = 32
PAD = 8
VMEM_LIMIT = 64 * 1024 * 1024


def _zero_pads(buf):
    extent_y, extent_z = buf.shape[1] - 2 * PAD, buf.shape[2]
    zeros = jnp.zeros((PAD, extent_z), jnp.float32)

    def body(p, carry):
        buf[p, pl.ds(0, PAD), :] = zeros
        buf[p, pl.ds(PAD + extent_y, PAD), :] = zeros
        return carry

    lax.fori_loop(0, buf.shape[0], body, 0)


def _plane_loop(first, last, extent_y, body):
    def step(i, carry):
        for y0 in range(0, extent_y, ROWS):
            body(first + i, y0)
        return carry

    lax.fori_loop(0, last - first, step, 0)


def _neighbour_sum(src, at, y0, kxo_lo, kxo_hi, kyl, kyh, kzl, kzh):
    extent_z = src.shape[2]
    center = src[at, pl.ds(PAD + y0, ROWS), :]
    below = src[at, pl.ds(PAD + y0 - 1, ROWS), :]
    above = src[at, pl.ds(PAD + y0 + 1, ROWS), :]
    lanes = lax.broadcasted_iota(jnp.int32, center.shape, 1)
    left = jnp.where(lanes == 0, 0.0, pltpu.roll(center, 1, 1))
    right = jnp.where(lanes == extent_z - 1, 0.0, pltpu.roll(center, extent_z - 1, 1))
    off = (
        kxo_lo * src[at - 1, pl.ds(PAD + y0, ROWS), :]
        + kxo_hi * src[at + 1, pl.ds(PAD + y0, ROWS), :]
        + kyl * below
        + kyh * above
        + kzl * left
        + kzh * right
    )
    return center, off


def _smooth_in_vmem(resid, kxo, kyl, kyh, kzl, kzh, w, out, bufs, sweeps):
    length, extent_y = resid.shape[0], resid.shape[1]
    for buf in bufs:
        _zero_pads(buf)

    def first(q, y0):
        rows = pl.ds(y0, ROWS)
        bufs[0][q, pl.ds(PAD + y0, ROWS), :] = w[q, rows, :] * resid[q, rows, :]

    _plane_loop(0, length, extent_y, first)
    for sweep_no in range(1, sweeps):
        src = bufs[(sweep_no - 1) % 2]
        src_at = sweep_no - 1
        last = sweep_no == sweeps - 1
        dst = out if last else bufs[sweep_no % 2]
        dst_at = sweep_no

        def body(q, y0, src=src, src_at=src_at, dst=dst, dst_at=dst_at, last=last):
            rows = pl.ds(y0, ROWS)
            center, off = _neighbour_sum(
                src, q - src_at, y0, kxo[q - 1, rows, :], kxo[q, rows, :],
                kyl[q, rows, :], kyh[q, rows, :], kzl[q, rows, :], kzh[q, rows, :],
            )
            new = (1.0 - OMEGA) * center + w[q, rows, :] * (resid[q, rows, :] + off)
            if last:
                dst[q - dst_at, rows, :] = new
            else:
                dst[q - dst_at, pl.ds(PAD + y0, ROWS), :] = new

        _plane_loop(sweep_no, length - sweep_no, extent_y, body)


def _fine_first_kernel(resid, kxo_full, kyl, kyh, kzl, kzh, w, out, low, high, buf_a, buf_b):
    _smooth_in_vmem(resid, kxo_full.at[1:-1], kyl, kyh, kzl, kzh, w, out, (buf_a, buf_b), SWEEPS)
    width, block, extent_y = low.shape[0], out.shape[0], out.shape[1]

    def edges(q, y0):
        rows = pl.ds(y0, ROWS)
        low[q, rows, :] = out[q, rows, :]
        high[q, rows, :] = out[block - width + q, rows, :]

    _plane_loop(0, width, extent_y, edges)


def _fine_second_kernel(
    fine_l, fine, fine_r, rhs, kxo_full, kyl, kyh, kzl, kzh, w, diag, out, resid_out, held, resid,
    buf_a, buf_b,
):
    width, block, extent_y = fine_l.shape[0], fine.shape[0], fine.shape[1]
    planes = held.shape[0]
    _zero_pads(held)
    for src, first in ((fine_l, 0), (fine, width), (fine_r, width + block)):

        def copy_in(q, y0, src=src, first=first):
            held[q, pl.ds(PAD + y0, ROWS), :] = src[q - first, pl.ds(y0, ROWS), :]

        _plane_loop(first, first + src.shape[0], extent_y, copy_in)

    def residual(q, y0):
        rows = pl.ds(y0, ROWS)
        center, off = _neighbour_sum(
            held, q + 1, y0, kxo_full[q, rows, :], kxo_full[q + 1, rows, :],
            kyl[q, rows, :], kyh[q, rows, :], kzl[q, rows, :], kzh[q, rows, :],
        )
        resid[q, rows, :] = rhs[q, rows, :] - (diag[q, rows, :] * center - off)

    _plane_loop(0, planes - 2, extent_y, residual)
    ghosts = SWEEPS - 1

    def copy_out(q, y0):
        rows = pl.ds(y0, ROWS)
        resid_out[q - ghosts, rows, :] = resid[q, rows, :]

    _plane_loop(ghosts, planes - 2 - ghosts, extent_y, copy_out)
    _smooth_in_vmem(
        resid, kxo_full.at[1:-1], kyl, kyh, kzl, kzh, w, out, (buf_a, buf_b), SWEEPS
    )


def _vmem_call(kernel, outs, scratch, *args):
    return pl.pallas_call(
        kernel,
        out_shape=outs,
        in_specs=[pl.BlockSpec(memory_space=pltpu.VMEM)] * len(args),
        out_specs=(
            [pl.BlockSpec(memory_space=pltpu.VMEM)] * len(outs)
            if isinstance(outs, (list, tuple))
            else pl.BlockSpec(memory_space=pltpu.VMEM)
        ),
        scratch_shapes=scratch,
        compiler_params=pltpu.CompilerParams(vmem_limit_bytes=VMEM_LIMIT),
    )(*args)


def fine_smooth(resid_ext, co, width):
    length, extent_y, extent_z = resid_ext.shape
    outs = [
        jax.ShapeDtypeStruct((length - 2 * (SWEEPS - 1), extent_y, extent_z), jnp.float32),
        jax.ShapeDtypeStruct((width, extent_y, extent_z), jnp.float32),
        jax.ShapeDtypeStruct((width, extent_y, extent_z), jnp.float32),
    ]
    padded = lambda planes: pltpu.VMEM((planes, extent_y + 2 * PAD, extent_z), jnp.float32)
    return _vmem_call(
        _fine_first_kernel, outs, [padded(length), padded(length - 2)],
        resid_ext, co["kxo"], co["kyl"], co["kyh"], co["kzl"], co["kzh"], co["w"],
    )


def fine_second(fine_l, fine, fine_r, rhs_ext, co):
    extent_y, extent_z = fine.shape[1], fine.shape[2]
    planes = fine.shape[0] + 2 * fine_l.shape[0]
    length = planes - 2
    block = length - 2 * (SWEEPS - 1)
    outs = [jax.ShapeDtypeStruct((block, extent_y, extent_z), jnp.float32)] * 2
    padded = lambda n: pltpu.VMEM((n, extent_y + 2 * PAD, extent_z), jnp.float32)
    return _vmem_call(
        _fine_second_kernel, outs,
        [padded(planes), pltpu.VMEM((length, extent_y, extent_z), jnp.float32),
         padded(length), padded(length - 2)],
        fine_l, fine, fine_r, rhs_ext, co["kxo"], co["kyl"], co["kyh"], co["kzl"], co["kzh"], co["w"], co["diag"],
    )


def per_device(right_side, density):
    me = lax.axis_index("gx")

    (dl, rl), (dr, rr) = exchange(
        [density[-3:], right_side[-2:]], [density[:3], right_side[:2]], 1
    )
    rho0_ext = jnp.concatenate([dl, density, dr])
    rhs_ext = jnp.concatenate([rl, right_side, rr])
    co0 = make_coefs(rho0_ext, 1.0)

    fine_0, low, high = fine_smooth(rhs_ext, co0, 3)

    (fl,), (fr,) = exchange([high], [low], 1)
    fine_1, resid_block = fine_second(fl, fine_0, fr, rhs_ext, co0)

    rho1 = coarsen(density)
    rho2 = coarsen(rho1)
    rho3 = coarsen(rho2)

    def restrict(resid):
        r1 = coarsen(resid)
        r2 = coarsen(r1)
        return r1, r2, coarsen(r2)

    cycles = [restrict(right_side), restrict(resid_block)]
    to_right, to_left = [], []
    for r1, r2, _ in cycles:
        to_right += [r1[-2:], r2]
        to_left += [r1[:2], r2]
    to_right += [rho1[-3:], rho2]
    to_left += [rho1[:3], rho2]
    level3 = jnp.concatenate([r3 for _, _, r3 in cycles] + [rho3])
    to_right.append(level3)
    to_left.append(level3)
    got_l, got_r = exchange(to_right, to_left, 1, True)
    parts = []
    for k, (r1, r2, _) in enumerate(cycles):
        r1e = jnp.concatenate([got_l[2 * k], r1, got_r[2 * k]])
        r2e = jnp.concatenate([got_l[2 * k + 1], r2, got_r[2 * k + 1]])
        parts.append((r1e * inside(4, 2, r1e.shape[0]), r2e * inside(2, 2, r2e.shape[0])))
    at = 2 * len(cycles)
    rho1e = jnp.concatenate([got_l[at], rho1, got_r[at]])
    rho2_l, rho2_r = got_l[at + 1], got_r[at + 1]
    win3 = jnp.concatenate([got_l[-1], level3, got_r[-1]])
    got_l, got_r = exchange([win3, rho2_r[-1:]], [win3, rho2_l[:1]], 3, True)
    win9 = jnp.concatenate([got_l[0], win3, got_r[0]])
    rho2e = jnp.concatenate([got_l[1], rho2_l, rho2, rho2_r, got_r[1]])
    (got_l,), (got_r,) = exchange([win9], [win9], 9, True)
    win27 = jnp.concatenate([got_l, win9, got_r])
    per = len(cycles) + 1
    win27 = win27.reshape(27, per, win27.shape[1], win27.shape[2]) * inside(1, 13, 27)[:, None]
    windows = [win27[:, k] for k in range(per)]
    rho3w = windows[-1]

    co1 = make_coefs(rho1e * inside(4, 3, rho1e.shape[0]), 0.25)
    co2 = make_coefs(rho2e * inside(2, 3, rho2e.shape[0]), 0.25**2)
    center = 13
    co3 = make_coefs(rho3w[center - 3:center + 4], 0.25**3)
    pair_start = 1 - me % 2

    def to_top(window):
        return coarsen(lax.dynamic_slice_in_dim(window, pair_start, 2 * center))

    co4 = make_coefs(to_top(rho3w), 0.25**4)

    def coarse_part(r1e, r2e, r3w):
        top = smooth(to_top(r3w)[1:-1], co4, TOP_SWEEPS)
        summed = grow_sides(top) + smooth(r3w[center - 2:center + 3], co3, SWEEPS)
        summed = refine(summed) + smooth(r2e, co2, SWEEPS)
        summed = refine(summed) + smooth(r1e, co1, SWEEPS)
        return refine(summed)

    coarse_0 = coarse_part(parts[0][0], parts[0][1], windows[0])
    coarse_1 = coarse_part(parts[1][0], parts[1][1], windows[1])
    pressure = (fine_0 + fine_1) + coarse_0
    return (pressure, coarse_1)


def solution(mesh):
    return jax.shard_map(
        per_device,
        mesh=mesh,
        in_specs=(P("gx", None, None), P("gx", None, None)),
        out_specs=(P("gx", None, None), P("gx", None, None)),
        check_vma=False,
    )
```
